512 devices in a mesh: front: 4 (over y), row: 4 (over x), col: 32 (over z, core).
Axes of the slice: x: 4, y: 4, z: 16, core: 2. Of those that a mesh axis runs over, the one named last changes fastest.
Arguments:
- inverse_factor: bfloat16 [4, 1024, 1024], P('front', ('row', 'col')), as said below
- panel: bfloat16 [4, 8192, 1024], P('front', 'row', 'col'), may hold values from -1.1953125 to 1.1953125
- trailing: float32 [4, 8192, 8192], P('front', 'row', 'col'), may hold values from -6 to 6
- extend_map: int32 [4, 512], P('front'), may hold values from 0 to 511, as said below
Outputs:
- parent_update: float32 [4, 4096, 8192], P('front', 'row', 'col')
The draws below stay inside these ranges and needn't reach their ends.
Inputs may be any that keep to these rules, and one draw needn't show every extreme that they name: Each inverse_factor[f] is upper triangular with positive diagonal. Each row of extend_map is a permutation of 0 to 511, and extend_map[f, q] % (128) == q % 128.
All inputs are finite; a program needn't handle non-finite values.
Results may differ from the reference program's by a relative error of at most 0.0034.
Values may be sent and summed in bfloat16 or wider, within the bound.
No kernel may reach another device: no remote copies, remote signals or barrier semaphores. Data moves between devices by JAX's collectives and lax.ppermute only.
A program may use at most 64 MiB of HBM per device.

```python
import jax
import jax.numpy as jnp
import numpy as np

ORDER = 8192
PANEL = 1024
BLOCK = 16
FRONTS = 4
NBLOCKS = 512
N_ROW = 4
N_COL = 32


def draw_inverse_factor(key, part):
    key_off, key_diag = jax.random.split(key, 2)
    upper_part = jax.random.normal(key_off, (FRONTS, PANEL, PANEL), jnp.float32) * (0.5 / PANEL ** 0.5)
    rows = jnp.arange(PANEL)[:, None]
    cols = jnp.arange(PANEL)[None, :]
    strict = (cols > rows).astype(jnp.float32)
    eye = (cols == rows).astype(jnp.float32)
    diag = 1.0 + jax.random.uniform(key_diag, (FRONTS, PANEL), jnp.float32, 0.0, 1.0)
    matrix = upper_part * strict[None] + eye[None] * diag[:, :, None]
    return matrix.astype(jnp.bfloat16)


def draw_extend_map(key, part):
    group = N_ROW * N_COL
    per_class = NBLOCKS // group
    position = jnp.arange(NBLOCKS, dtype=jnp.int32)
    scores = jax.random.randint(key, (FRONTS, NBLOCKS), 0, 4096)
    total = (position % group)[None, :] * (4096 * NBLOCKS) + scores * NBLOCKS + position[None, :]
    order = jnp.argsort(total, axis=1)
    values = position % per_class * group + position // per_class
    fronts = jnp.arange(FRONTS, dtype=jnp.int32)[:, None] + 0 * order
    result = jnp.zeros((FRONTS, NBLOCKS), jnp.int32)
    return result.at[fronts, order].set(values[None, :] + 0 * order)


def shard_levels(key, extent, cuts, smallest, top_value):
    loudness, own = 1.0, jax.random.fold_in(key, 6)
    for dim, blocks in cuts:
        steps = jnp.exp(jax.random.uniform(jax.random.fold_in(own, dim), (blocks,), jnp.float32, smallest / len(cuts), top_value / len(cuts)))
        loudness = loudness * jnp.repeat(steps, extent[dim] // blocks).reshape([-1 if axis == dim else 1 for axis in range(len(extent))])
    return loudness


def normal_values(own_key, shape, spread, reach, pieces=(), kind=jnp.bfloat16):
    array = jax.random.normal(own_key, shape, jnp.float32) * spread
    if len(pieces) > 0:
        array = shard_levels(own_key, shape, pieces, -0.22, 0.18) * array
    return jnp.clip(array, min=-reach, max=reach).astype(kind)


def setup_inputs(seed: int = 0) -> dict:
    key_of = jax.random.split(jax.random.key(seed), 5)
    return {
        "inverse_factor": draw_inverse_factor(jax.random.fold_in(key_of[4], 71), 0),
        "panel": normal_values(key_of[1], (FRONTS, ORDER, PANEL), 0.2, 1.1953125, ((0, 4), (1, 4), (2, 32))),
        "trailing": normal_values(key_of[2], (FRONTS, ORDER, ORDER), 1.0, 6.0, ((0, 4), (1, 4), (2, 32)), jnp.float32),
        "extend_map": draw_extend_map(jax.random.fold_in(key_of[4], 71), 0),
    }


def storage_positions():
    group = N_ROW * N_COL
    per_class = NBLOCKS // group
    index = np.arange(ORDER)
    within = index % BLOCK
    blocks = index // BLOCK
    row_of = blocks % N_ROW
    col_of = (blocks // N_ROW) % N_COL
    depth = blocks // group
    row_pos = ((row_of * N_COL + col_of) * per_class + depth) * BLOCK + within
    col_pos = ((col_of * N_ROW + row_of) * per_class + depth) * BLOCK + within
    return row_pos, col_pos


def child_update(inverse, panel_rows, trailing_block, block_map, row_pos, col_pos):
    logical_panel = panel_rows[row_pos]
    lower = jnp.dot(logical_panel, inverse, preferred_element_type=jnp.float32)
    rounded = lower.astype(jnp.bfloat16)
    logical = trailing_block[row_pos][:, col_pos]
    schur = logical - jnp.dot(rounded, rounded.T, preferred_element_type=jnp.float32)
    index = jnp.arange(ORDER).astype(jnp.int32)
    parent_index = (block_map[index // BLOCK] * BLOCK + index % BLOCK).astype(jnp.int32)
    inverse_order = jnp.argsort(parent_index)
    return schur[inverse_order][:, inverse_order]


def reference(inverse_factor, panel, trailing, extend_map):
    row_pos, col_pos = storage_positions()
    row_back = np.argsort(row_pos)
    col_back = np.argsort(col_pos)
    halves = []
    for pair in range(FRONTS // 2):
        total = child_update(inverse_factor[2 * pair], panel[2 * pair], trailing[2 * pair], extend_map[2 * pair], row_pos, col_pos)
        total = total + child_update(inverse_factor[2 * pair + 1], panel[2 * pair + 1], trailing[2 * pair + 1], extend_map[2 * pair + 1], row_pos, col_pos)
        stored = total[row_back][:, col_back]
        shaped = stored.reshape(N_ROW, 2, ORDER // (2 * N_ROW), ORDER)
        for member in range(2):
            halves.append(shaped[:, member].reshape(ORDER // 2, ORDER))
    return jnp.stack(halves)
```

```python
import jax
import jax.numpy as jnp
from jax import lax
from jax.sharding import Mesh
from jax.sharding import PartitionSpec as P


def from_partner(value, axis, distance):
    mask = 2**distance
    pairs = [(source, source ^ mask) for source in range(lax.axis_size(axis))]
    return lax.ppermute(value, axis, pairs)


def outer_rows(left, right):
    return lax.dot_general(
        left, right, (((1,), (1,)), ((), ())), preferred_element_type=jnp.float32
    )


def local(inverse_factor, panel, trailing, extend_map):
    nrow = lax.axis_size("row")
    nz = lax.axis_size("z")
    ncore = lax.axis_size("core")
    ncol = nz * ncore
    group = nrow * ncol
    row_index = lax.axis_index("row")
    col_index = lax.axis_index("z") * ncore + lax.axis_index("core")

    inverse = lax.all_gather(inverse_factor[0], "core", axis=0, tiled=True)
    inverse = lax.all_gather(inverse, "z", axis=0, tiled=True)
    inverse = lax.all_gather(inverse, "row", axis=0, tiled=True)
    order = inverse.shape[0]
    chunk = order // ncol
    inverse = (
        inverse.reshape(nz, ncore, chunk, order)
        .transpose(1, 0, 2, 3)
        .reshape(order, order)
    )

    columns = lax.all_gather(panel[0], "z", axis=1, tiled=True)
    columns = lax.all_gather(columns, "core", axis=1, tiled=True)
    solved = jnp.dot(columns, inverse, preferred_element_type=jnp.float32).astype(
        jnp.bfloat16
    )

    local_trailing = trailing[0]
    rows_here = local_trailing.shape[0]
    cols_here = local_trailing.shape[1]
    share = rows_here // ncol
    piece = lax.dynamic_slice_in_dim(solved, col_index * share, share, 0)
    col_side = lax.all_gather(piece, "row", axis=0, tiled=True)

    block_map = extend_map[0]
    nblocks = block_map.shape[0]
    per_class = nblocks // group
    width = rows_here // (ncol * per_class)
    slots_row = jnp.arange(ncol * per_class, dtype=jnp.int32)
    class_row = slots_row // per_class
    depth_row = slots_row % per_class
    source_row = (depth_row * ncol + class_row) * nrow + row_index
    target_row = class_row * per_class + block_map[source_row] // group
    gather_row = jnp.argsort(target_row)
    slots_col = jnp.arange(nrow * per_class, dtype=jnp.int32)
    class_col = slots_col // per_class
    depth_col = slots_col % per_class
    source_col = (depth_col * ncol + col_index) * nrow + class_col
    target_col = class_col * per_class + block_map[source_col] // group
    gather_col = jnp.argsort(target_col)

    col_side = col_side.reshape(nrow * per_class, width, order)[gather_col].reshape(
        cols_here, order
    )
    lane = jnp.arange(cols_here, dtype=jnp.int32)
    picked = gather_col[lane // width] * width + lane % width
    select_cols = (lane[:, None] == picked[None, :]).astype(jnp.float32)

    member = lax.axis_index("front") % 2
    half = rows_here // 2
    half_blocks = half // width

    def half_update(which):
        rows = lax.dynamic_slice_in_dim(local_trailing, which * half, half, 0)
        low = lax.dynamic_slice_in_dim(solved, which * half, half, 0)
        moved_cols = jnp.dot(
            rows,
            select_cols,
            precision=lax.Precision.HIGHEST,
            preferred_element_type=jnp.float32,
        )
        schur = moved_cols - outer_rows(low, col_side)
        blocks = (
            lax.dynamic_slice_in_dim(gather_row, which * half_blocks, half_blocks, 0)
            - which * half_blocks
        )
        return schur.reshape(half_blocks, width, cols_here)[blocks].reshape(
            half, cols_here
        )

    outgoing = half_update(1 - member)
    incoming = from_partner(outgoing, "front", 0)
    keep = half_update(member)
    return (keep + incoming)[None]


def solution(mesh):
    devices = mesh.devices
    shape = devices.shape
    fine = Mesh(
        devices.reshape(shape[0], shape[1], shape[2] // 2, 2),
        ("front", "row", "z", "core"),
    )
    cols = ("z", "core")
    return jax.shard_map(
        local,
        mesh=fine,
        in_specs=(
            P("front", ("row",) + cols, None),
            P("front", "row", cols),
            P("front", "row", cols),
            P("front", None),
        ),
        out_specs=P("front", "row", cols),
        check_vma=False,
    )
```

```python
import jax
import jax.numpy as jnp
from jax import lax
from jax.sharding import Mesh
from jax.sharding import PartitionSpec as P


def from_partner(value, axis, distance):
    mask = 2**distance
    pairs = [(source, source ^ mask) for source in range(lax.axis_size(axis))]
    return lax.ppermute(value, axis, pairs)


def outer_rows(left, right):
    return lax.dot_general(
        left, right, (((1,), (1,)), ((), ())), preferred_element_type=jnp.float32
    )


def ring_gather(value, axis, index, n):
    ahead = [(source, (source + 1) % n) for source in range(n)]
    behind = [(source, (source - 1) % n) for source in range(n)]
    held = [value]
    forward = value
    backward = value
    for step in range(1, n):
        if step % 2:
            forward = lax.ppermute(forward, axis, ahead)
            held.append(forward)
        else:
            backward = lax.ppermute(backward, axis, behind)
            held.append(backward)
    offsets = [0] + [(step + 1) // 2 if step % 2 else -(step // 2) for step in range(1, n)]
    by_offset = [None] * n
    for offset, block in zip(offsets, held):
        by_offset[offset % n] = block
    stacked = jnp.stack(by_offset)
    sources = jnp.arange(n, dtype=jnp.int32)
    return stacked[(index - sources) % n]


def local(inverse_factor, panel, trailing, extend_map):
    nrow = lax.axis_size("row")
    nz = lax.axis_size("z")
    ncore = lax.axis_size("core")
    ncol = nz * ncore
    group = nrow * ncol
    row_index = lax.axis_index("row")
    col_index = lax.axis_index("z") * ncore + lax.axis_index("core")

    inverse = lax.all_gather(inverse_factor[0], "core", axis=0, tiled=True)
    inverse = lax.all_gather(inverse, "z", axis=0, tiled=True)
    inverse = ring_gather(inverse, "row", row_index, nrow)
    order = inverse.shape[-1]
    inverse = inverse.reshape(order, order)

    columns = lax.all_gather(panel[0], ("z", "core"), axis=1, tiled=True)

    def solve(rows):
        return jnp.dot(rows, inverse, preferred_element_type=jnp.float32).astype(
            jnp.bfloat16
        )

    local_trailing = trailing[0]
    rows_here = local_trailing.shape[0]
    cols_here = local_trailing.shape[1]
    share = rows_here // ncol
    piece = solve(lax.dynamic_slice_in_dim(columns, col_index * share, share, 0))
    col_side = ring_gather(piece, "row", row_index, nrow)

    block_map = extend_map[0]
    nblocks = block_map.shape[0]
    per_class = nblocks // group
    width = rows_here // (ncol * per_class)
    slots_row = jnp.arange(ncol * per_class, dtype=jnp.int32)
    class_row = slots_row // per_class
    depth_row = slots_row % per_class
    source_row = (depth_row * ncol + class_row) * nrow + row_index
    target_row = class_row * per_class + block_map[source_row] // group
    gather_row = jnp.argsort(target_row)
    slots_col = jnp.arange(nrow * per_class, dtype=jnp.int32)
    class_col = slots_col // per_class
    depth_col = slots_col % per_class
    source_col = (depth_col * ncol + col_index) * nrow + class_col
    target_col = class_col * per_class + block_map[source_col] // group
    gather_col = jnp.argsort(target_col)

    col_side = col_side.reshape(nrow * per_class, width, order)[gather_col].reshape(
        cols_here, order
    )
    lane = jnp.arange(cols_here, dtype=jnp.int32)
    picked = gather_col[lane // width] * width + lane % width
    select_cols = (lane[:, None] == picked[None, :]).astype(jnp.float32)

    member = lax.axis_index("front") % 2
    half = rows_here // 2
    half_blocks = half // width

    def half_update(which):
        rows = lax.dynamic_slice_in_dim(local_trailing, which * half, half, 0)
        low = solve(lax.dynamic_slice_in_dim(columns, which * half, half, 0))
        moved_cols = jnp.dot(
            rows,
            select_cols,
            precision=lax.Precision.HIGHEST,
            preferred_element_type=jnp.float32,
        )
        schur = moved_cols - outer_rows(low, col_side)
        blocks = (
            lax.dynamic_slice_in_dim(gather_row, which * half_blocks, half_blocks, 0)
            - which * half_blocks
        )
        return schur.reshape(half_blocks, width, cols_here)[blocks].reshape(
            half, cols_here
        )

    outgoing = half_update(1 - member)
    incoming = from_partner(outgoing, "front", 0)
    keep = half_update(member)
    return (keep + incoming)[None]


def solution(mesh):
    devices = mesh.devices
    shape = devices.shape
    fine = Mesh(
        devices.reshape(shape[0], shape[1], shape[2] // 2, 2),
        ("front", "row", "z", "core"),
    )
    cols = ("z", "core")
    return jax.shard_map(
        local,
        mesh=fine,
        in_specs=(
            P("front", ("row",) + cols, None),
            P("front", "row", cols),
            P("front", "row", cols),
            P("front", None),
        ),
        out_specs=P("front", "row", cols),
        check_vma=False,
    )
```

```python
import jax
import jax.numpy as jnp
from jax import lax
from jax.sharding import Mesh
from jax.sharding import PartitionSpec as P


def from_partner(value, axis, distance):
    mask = 2**distance
    pairs = [(source, source ^ mask) for source in range(lax.axis_size(axis))]
    return lax.ppermute(value, axis, pairs)


def outer_rows(left, right):
    return lax.dot_general(
        left, right, (((1,), (1,)), ((), ())), preferred_element_type=jnp.float32
    )


def ring_gather(value, axis, index, n):
    ahead = [(source, (source + 1) % n) for source in range(n)]
    behind = [(source, (source - 1) % n) for source in range(n)]
    held = [value]
    forward = value
    backward = value
    for step in range(1, n):
        if step % 2:
            forward = lax.ppermute(forward, axis, ahead)
            held.append(forward)
        else:
            backward = lax.ppermute(backward, axis, behind)
            held.append(backward)
    offsets = [0] + [(step + 1) // 2 if step % 2 else -(step // 2) for step in range(1, n)]
    by_offset = [None] * n
    for offset, block in zip(offsets, held):
        by_offset[offset % n] = block
    stacked = jnp.stack(by_offset)
    sources = jnp.arange(n, dtype=jnp.int32)
    return stacked[(index - sources) % n]


def local(inverse_factor, panel, trailing, extend_map):
    nrow = lax.axis_size("row")
    nz = lax.axis_size("z")
    ncore = lax.axis_size("core")
    ncol = nz * ncore
    group = nrow * ncol
    row_index = lax.axis_index("row")
    col_index = lax.axis_index("z") * ncore + lax.axis_index("core")

    inverse = lax.all_gather(inverse_factor[0], "core", axis=0, tiled=True)
    inverse = lax.all_gather(inverse, "z", axis=0, tiled=True)
    inverse = ring_gather(inverse, "row", row_index, nrow)
    order = inverse.shape[-1]
    inverse = inverse.reshape(order, order)

    def solve(rows):
        return jnp.dot(rows, inverse, preferred_element_type=jnp.float32).astype(
            jnp.bfloat16
        )

    local_panel = panel[0]
    local_trailing = trailing[0]
    rows_here = local_trailing.shape[0]
    cols_here = local_trailing.shape[1]
    member = lax.axis_index("front") % 2
    half = rows_here // 2
    cols = ("z", "core")
    piece_panel = lax.all_to_all(local_panel, cols, 0, 1, tiled=True)
    col_side = solve(ring_gather(piece_panel, "row", row_index, nrow).reshape(-1, order))
    away = lax.dynamic_slice_in_dim(local_panel, (1 - member) * half, half, 0)
    away = lax.all_gather(away, cols, axis=1, tiled=True)
    home = lax.dynamic_slice_in_dim(local_panel, member * half, half, 0)
    home = lax.all_gather(home, cols, axis=1, tiled=True)

    block_map = extend_map[0]
    nblocks = block_map.shape[0]
    per_class = nblocks // group
    width = rows_here // (ncol * per_class)
    slots_row = jnp.arange(ncol * per_class, dtype=jnp.int32)
    class_row = slots_row // per_class
    depth_row = slots_row % per_class
    source_row = (depth_row * ncol + class_row) * nrow + row_index
    target_row = class_row * per_class + block_map[source_row] // group
    gather_row = jnp.argsort(target_row)
    slots_col = jnp.arange(nrow * per_class, dtype=jnp.int32)
    class_col = slots_col // per_class
    depth_col = slots_col % per_class
    source_col = (depth_col * ncol + col_index) * nrow + class_col
    target_col = class_col * per_class + block_map[source_col] // group
    gather_col = jnp.argsort(target_col)

    col_side = col_side.reshape(nrow * per_class, width, order)[gather_col].reshape(
        cols_here, order
    )
    lane = jnp.arange(cols_here, dtype=jnp.int32)
    picked = gather_col[lane // width] * width + lane % width
    select_cols = (lane[:, None] == picked[None, :]).astype(jnp.float32)

    half_blocks = half // width

    def half_update(which, columns):
        rows = lax.dynamic_slice_in_dim(local_trailing, which * half, half, 0)
        low = solve(columns)
        moved_cols = jnp.dot(
            rows,
            select_cols,
            precision=lax.Precision.HIGHEST,
            preferred_element_type=jnp.float32,
        )
        schur = moved_cols - outer_rows(low, col_side)
        blocks = (
            lax.dynamic_slice_in_dim(gather_row, which * half_blocks, half_blocks, 0)
            - which * half_blocks
        )
        return schur.reshape(half_blocks, width, cols_here)[blocks].reshape(
            half, cols_here
        )

    outgoing = half_update(1 - member, away).astype(jnp.bfloat16)
    incoming = from_partner(outgoing, "front", 0)
    keep = half_update(member, home)
    return (keep + incoming.astype(jnp.float32))[None]


def solution(mesh):
    devices = mesh.devices
    shape = devices.shape
    fine = Mesh(
        devices.reshape(shape[0], shape[1], shape[2] // 2, 2),
        ("front", "row", "z", "core"),
    )
    cols = ("z", "core")
    return jax.shard_map(
        local,
        mesh=fine,
        in_specs=(
            P("front", ("row",) + cols, None),
            P("front", "row", cols),
            P("front", "row", cols),
            P("front", None),
        ),
        out_specs=P("front", "row", cols),
        check_vma=False,
    )
```

```python
import jax
import jax.numpy as jnp
from jax import lax
from jax.sharding import Mesh
from jax.sharding import PartitionSpec as P


def from_partner(value, axis, distance):
    mask = 2**distance
    pairs = [(source, source ^ mask) for source in range(lax.axis_size(axis))]
    return lax.ppermute(value, axis, pairs)


def outer_rows(left, right):
    return lax.dot_general(
        left, right, (((1,), (1,)), ((), ())), preferred_element_type=jnp.float32
    )


def local(inverse_factor, panel, trailing, extend_map):
    nrow = lax.axis_size("row")
    nz = lax.axis_size("z")
    ncore = lax.axis_size("core")
    ncol = nz * ncore
    group = nrow * ncol
    row_index = lax.axis_index("row")
    col_index = lax.axis_index("z") * ncore + lax.axis_index("core")

    local_panel = panel[0]
    local_trailing = trailing[0]
    rows_here = local_trailing.shape[0]
    cols_here = local_trailing.shape[1]
    chunk = local_panel.shape[1]
    cols = ("z", "core")

    inverse = lax.all_gather(inverse_factor[0], "row", axis=0, tiled=True)
    order = inverse.shape[1]
    held = inverse.shape[0]
    payload = jnp.concatenate([local_panel, inverse.reshape(-1, chunk)], axis=0)
    gathered = lax.all_gather(payload, cols, axis=1, tiled=True)
    columns = gathered[:rows_here]
    inverse = (
        gathered[rows_here:]
        .reshape(nrow, held // nrow, order // chunk, ncol, chunk)
        .transpose(0, 3, 1, 2, 4)
        .reshape(order, order)
    )

    def solve(rows):
        return jnp.dot(rows, inverse, preferred_element_type=jnp.float32).astype(
            jnp.bfloat16
        )

    member = lax.axis_index("front") % 2
    half = rows_here // 2
    piece_panel = lax.all_to_all(local_panel, cols, 0, 1, tiled=True)
    col_side = solve(lax.all_gather(piece_panel, "row", axis=0, tiled=True))
    away = lax.dynamic_slice_in_dim(columns, (1 - member) * half, half, 0)
    home = lax.dynamic_slice_in_dim(columns, member * half, half, 0)

    block_map = extend_map[0]
    nblocks = block_map.shape[0]
    per_class = nblocks // group
    width = rows_here // (ncol * per_class)
    slots_row = jnp.arange(ncol * per_class, dtype=jnp.int32)
    class_row = slots_row // per_class
    depth_row = slots_row % per_class
    source_row = (depth_row * ncol + class_row) * nrow + row_index
    target_row = class_row * per_class + block_map[source_row] // group
    gather_row = jnp.argsort(target_row)
    slots_col = jnp.arange(nrow * per_class, dtype=jnp.int32)
    class_col = slots_col // per_class
    depth_col = slots_col % per_class
    source_col = (depth_col * ncol + col_index) * nrow + class_col
    target_col = class_col * per_class + block_map[source_col] // group
    gather_col = jnp.argsort(target_col)

    col_side = col_side.reshape(nrow * per_class, width, order)[gather_col].reshape(
        cols_here, order
    )
    lane = jnp.arange(cols_here, dtype=jnp.int32)
    picked = gather_col[lane // width] * width + lane % width
    select_cols = (lane[:, None] == picked[None, :]).astype(jnp.float32)

    half_blocks = half // width

    def half_update(which, columns):
        rows = lax.dynamic_slice_in_dim(local_trailing, which * half, half, 0)
        low = solve(columns)
        moved_cols = jnp.dot(
            rows,
            select_cols,
            precision=lax.Precision.HIGHEST,
            preferred_element_type=jnp.float32,
        )
        schur = moved_cols - outer_rows(low, col_side)
        blocks = (
            lax.dynamic_slice_in_dim(gather_row, which * half_blocks, half_blocks, 0)
            - which * half_blocks
        )
        return schur.reshape(half_blocks, width, cols_here)[blocks].reshape(
            half, cols_here
        )

    outgoing = half_update(1 - member, away).astype(jnp.bfloat16)
    incoming = from_partner(outgoing, "front", 0)
    keep = half_update(member, home)
    return (keep + incoming.astype(jnp.float32))[None]


def solution(mesh):
    devices = mesh.devices
    shape = devices.shape
    fine = Mesh(
        devices.reshape(shape[0], shape[1], shape[2] // 2, 2),
        ("front", "row", "z", "core"),
    )
    cols = ("z", "core")
    return jax.shard_map(
        local,
        mesh=fine,
        in_specs=(
            P("front", ("row",) + cols, None),
            P("front", "row", cols),
            P("front", "row", cols),
            P("front", None),
        ),
        out_specs=P("front", "row", cols),
        check_vma=False,
    )
```

```python
import jax
import jax.numpy as jnp
from jax import lax
from jax.sharding import Mesh
from jax.sharding import PartitionSpec as P


def from_partner(value, axis, distance):
    mask = 2**distance
    pairs = [(source, source ^ mask) for source in range(lax.axis_size(axis))]
    return lax.ppermute(value, axis, pairs)


def outer_rows(left, right):
    return lax.dot_general(
        left, right, (((1,), (1,)), ((), ())), preferred_element_type=jnp.float32
    )


def ring_gather(value, axis, index, n):
    ahead = [(source, (source + 1) % n) for source in range(n)]
    behind = [(source, (source - 1) % n) for source in range(n)]
    held = [value]
    forward = value
    backward = value
    for step in range(1, n):
        if step % 2:
            forward = lax.ppermute(forward, axis, ahead)
            held.append(forward)
        else:
            backward = lax.ppermute(backward, axis, behind)
            held.append(backward)
    offsets = [0] + [(step + 1) // 2 if step % 2 else -(step // 2) for step in range(1, n)]
    by_offset = [None] * n
    for offset, block in zip(offsets, held):
        by_offset[offset % n] = block
    stacked = jnp.stack(by_offset)
    sources = jnp.arange(n, dtype=jnp.int32)
    return stacked[(index - sources) % n]


def local(inverse_factor, panel, trailing, extend_map):
    nrow = lax.axis_size("row")
    nz = lax.axis_size("z")
    ncore = lax.axis_size("core")
    ncol = nz * ncore
    group = nrow * ncol
    row_index = lax.axis_index("row")
    col_index = lax.axis_index("z") * ncore + lax.axis_index("core")

    inverse = lax.all_gather(inverse_factor[0], "core", axis=0, tiled=True)
    inverse = lax.all_gather(inverse, "z", axis=0, tiled=True)
    inverse = ring_gather(inverse, "row", row_index, nrow)
    order = inverse.shape[-1]
    inverse = inverse.reshape(order, order)

    columns = lax.all_gather(panel[0], ("z", "core"), axis=1, tiled=True)

    def solve(rows):
        return jnp.dot(rows, inverse, preferred_element_type=jnp.float32).astype(
            jnp.bfloat16
        )

    local_trailing = trailing[0]
    rows_here = local_trailing.shape[0]
    cols_here = local_trailing.shape[1]
    share = rows_here // ncol
    piece = solve(lax.dynamic_slice_in_dim(columns, col_index * share, share, 0))
    col_side = ring_gather(piece, "row", row_index, nrow)

    block_map = extend_map[0]
    nblocks = block_map.shape[0]
    per_class = nblocks // group
    width = rows_here // (ncol * per_class)
    slots_row = jnp.arange(ncol * per_class, dtype=jnp.int32)
    class_row = slots_row // per_class
    depth_row = slots_row % per_class
    source_row = (depth_row * ncol + class_row) * nrow + row_index
    target_row = class_row * per_class + block_map[source_row] // group
    gather_row = jnp.argsort(target_row)
    slots_col = jnp.arange(nrow * per_class, dtype=jnp.int32)
    class_col = slots_col // per_class
    depth_col = slots_col % per_class
    source_col = (depth_col * ncol + col_index) * nrow + class_col
    target_col = class_col * per_class + block_map[source_col] // group
    gather_col = jnp.argsort(target_col)

    col_side = col_side.reshape(nrow * per_class, width, order)[gather_col].reshape(
        cols_here, order
    )
    lane = jnp.arange(cols_here, dtype=jnp.int32)
    picked = gather_col[lane // width] * width + lane % width
    select_cols = (lane[:, None] == picked[None, :]).astype(jnp.float32)

    member = lax.axis_index("front") % 2
    half = rows_here // 2
    half_blocks = half // width

    def half_update(which):
        rows = lax.dynamic_slice_in_dim(local_trailing, which * half, half, 0)
        low = solve(lax.dynamic_slice_in_dim(columns, which * half, half, 0))
        rows, low = lax.optimization_barrier((rows, low))
        moved_cols = jnp.dot(
            rows,
            select_cols,
            precision=lax.Precision.HIGHEST,
            preferred_element_type=jnp.float32,
        )
        schur = moved_cols - outer_rows(low, col_side)
        blocks = (
            lax.dynamic_slice_in_dim(gather_row, which * half_blocks, half_blocks, 0)
            - which * half_blocks
        )
        return schur.reshape(half_blocks, width, cols_here)[blocks].reshape(
            half, cols_here
        )

    outgoing = half_update(1 - member).astype(jnp.bfloat16)
    incoming = from_partner(outgoing, "front", 0)
    keep = half_update(member)
    return (keep + incoming.astype(jnp.float32))[None]


def solution(mesh):
    devices = mesh.devices
    shape = devices.shape
    fine = Mesh(
        devices.reshape(shape[0], shape[1], shape[2] // 2, 2),
        ("front", "row", "z", "core"),
    )
    cols = ("z", "core")
    return jax.shard_map(
        local,
        mesh=fine,
        in_specs=(
            P("front", ("row",) + cols, None),
            P("front", "row", cols),
            P("front", "row", cols),
            P("front", None),
        ),
        out_specs=P("front", "row", cols),
        check_vma=False,
    )
```

```python
import jax
import jax.numpy as jnp
from jax import lax
from jax.sharding import Mesh
from jax.sharding import PartitionSpec as P


def from_partner(value, axis, distance):
    mask = 2**distance
    pairs = [(source, source ^ mask) for source in range(lax.axis_size(axis))]
    return lax.ppermute(value, axis, pairs)


def outer_rows(left, right):
    return lax.dot_general(
        left, right, (((1,), (1,)), ((), ())), preferred_element_type=jnp.float32
    )


def ring_gather(value, axis, index, n):
    ahead = [(source, (source + 1) % n) for source in range(n)]
    behind = [(source, (source - 1) % n) for source in range(n)]
    held = [value]
    forward = value
    backward = value
    for step in range(1, n):
        if step % 2:
            forward = lax.ppermute(forward, axis, ahead)
            held.append(forward)
        else:
            backward = lax.ppermute(backward, axis, behind)
            held.append(backward)
    offsets = [0] + [(step + 1) // 2 if step % 2 else -(step // 2) for step in range(1, n)]
    by_offset = [None] * n
    for offset, block in zip(offsets, held):
        by_offset[offset % n] = block
    stacked = jnp.stack(by_offset)
    sources = jnp.arange(n, dtype=jnp.int32)
    return stacked[(index - sources) % n]


def inverse_order(target):
    slots = jnp.arange(target.shape[0], dtype=jnp.int32)
    hit = target[None, :] == slots[:, None]
    return jnp.sum(jnp.where(hit, slots[None, :], 0), axis=1, dtype=jnp.int32)


def local(inverse_factor, panel, trailing, extend_map):
    nrow = lax.axis_size("row")
    nz = lax.axis_size("z")
    ncore = lax.axis_size("core")
    ncol = nz * ncore
    group = nrow * ncol
    row_index = lax.axis_index("row")
    col_index = lax.axis_index("z") * ncore + lax.axis_index("core")

    inverse = lax.all_gather(inverse_factor[0], "core", axis=0, tiled=True)
    inverse = lax.all_gather(inverse, "z", axis=0, tiled=True)
    inverse = ring_gather(inverse, "row", row_index, nrow)
    order = inverse.shape[-1]
    inverse = inverse.reshape(order, order)

    columns = lax.all_gather(panel[0], ("z", "core"), axis=1, tiled=True)

    def solve(rows):
        return jnp.dot(rows, inverse, preferred_element_type=jnp.float32).astype(
            jnp.bfloat16
        )

    local_trailing = trailing[0]
    rows_here = local_trailing.shape[0]
    cols_here = local_trailing.shape[1]
    piece_panel = lax.all_to_all(panel[0], ("z", "core"), 0, 1, tiled=True)
    piece_panel = lax.all_gather(piece_panel, "row", axis=0, tiled=True)

    block_map = extend_map[0]
    nblocks = block_map.shape[0]
    per_class = nblocks // group
    width = rows_here // (ncol * per_class)
    slots_row = jnp.arange(ncol * per_class, dtype=jnp.int32)
    class_row = slots_row // per_class
    depth_row = slots_row % per_class
    source_row = (depth_row * ncol + class_row) * nrow + row_index
    target_row = class_row * per_class + block_map[source_row] // group
    gather_row = inverse_order(target_row)
    slots_col = jnp.arange(nrow * per_class, dtype=jnp.int32)
    class_col = slots_col // per_class
    depth_col = slots_col % per_class
    source_col = (depth_col * ncol + col_index) * nrow + class_col
    target_col = class_col * per_class + block_map[source_col] // group
    gather_col = inverse_order(target_col)

    col_side = solve(piece_panel)
    col_side = col_side.reshape(nrow * per_class, width, order)[gather_col].reshape(
        cols_here, order
    )
    blocks_col = slots_col[:, None] == gather_col[None, :]
    same = jnp.arange(width)[:, None] == jnp.arange(width)[None, :]
    select_cols = (blocks_col[:, None, :, None] & same[None, :, None, :]).reshape(
        cols_here, cols_here
    ).astype(jnp.float32)

    member = lax.axis_index("front") % 2
    half = rows_here // 2
    half_blocks = half // width

    def half_update(which):
        rows = lax.dynamic_slice_in_dim(local_trailing, which * half, half, 0)
        low = solve(lax.dynamic_slice_in_dim(columns, which * half, half, 0))
        rows, low = lax.optimization_barrier((rows, low))
        moved_cols = jnp.dot(
            rows,
            select_cols,
            precision=lax.Precision.HIGHEST,
            preferred_element_type=jnp.float32,
        )
        schur = moved_cols - outer_rows(low, col_side)
        blocks = (
            lax.dynamic_slice_in_dim(gather_row, which * half_blocks, half_blocks, 0)
            - which * half_blocks
        )
        return schur.reshape(half_blocks, width, cols_here)[blocks].reshape(
            half, cols_here
        )

    outgoing = half_update(1 - member).astype(jnp.bfloat16)
    incoming = from_partner(outgoing, "front", 0)
    keep = half_update(member)
    return (keep + incoming.astype(jnp.float32))[None]


def solution(mesh):
    devices = mesh.devices
    shape = devices.shape
    fine = Mesh(
        devices.reshape(shape[0], shape[1], shape[2] // 2, 2),
        ("front", "row", "z", "core"),
    )
    cols = ("z", "core")
    return jax.shard_map(
        local,
        mesh=fine,
        in_specs=(
            P("front", ("row",) + cols, None),
            P("front", "row", cols),
            P("front", "row", cols),
            P("front", None),
        ),
        out_specs=P("front", "row", cols),
        check_vma=False,
    )
```

```python
import jax
import jax.numpy as jnp
from jax import lax
from jax.sharding import Mesh
from jax.sharding import PartitionSpec as P


def from_partner(value, axis, distance):
    mask = 2**distance
    pairs = [(source, source ^ mask) for source in range(lax.axis_size(axis))]
    return lax.ppermute(value, axis, pairs)


def outer_rows(left, right):
    return lax.dot_general(
        left, right, (((1,), (1,)), ((), ())), preferred_element_type=jnp.float32
    )


def ring_gather(value, axis, index, n):
    ahead = [(source, (source + 1) % n) for source in range(n)]
    behind = [(source, (source - 1) % n) for source in range(n)]
    held = [value]
    forward = value
    backward = value
    for step in range(1, n):
        if step % 2:
            forward = lax.ppermute(forward, axis, ahead)
            held.append(forward)
        else:
            backward = lax.ppermute(backward, axis, behind)
            held.append(backward)
    offsets = [0] + [(step + 1) // 2 if step % 2 else -(step // 2) for step in range(1, n)]
    by_offset = [None] * n
    for offset, block in zip(offsets, held):
        by_offset[offset % n] = block
    stacked = jnp.stack(by_offset)
    sources = jnp.arange(n, dtype=jnp.int32)
    return stacked[(index - sources) % n]


def inverse_order(target):
    slots = jnp.arange(target.shape[0], dtype=jnp.int32)
    hit = target[None, :] == slots[:, None]
    return jnp.sum(jnp.where(hit, slots[None, :], 0), axis=1, dtype=jnp.int32)


def local(inverse_factor, panel, trailing, extend_map):
    nrow = lax.axis_size("row")
    nz = lax.axis_size("z")
    ncore = lax.axis_size("core")
    ncol = nz * ncore
    group = nrow * ncol
    row_index = lax.axis_index("row")
    col_index = lax.axis_index("z") * ncore + lax.axis_index("core")

    inverse = lax.all_gather(inverse_factor[0], "core", axis=0, tiled=True)
    inverse = lax.all_gather(inverse, "z", axis=0, tiled=True)
    inverse = ring_gather(inverse, "row", row_index, nrow)
    order = inverse.shape[-1]
    inverse = inverse.reshape(order, order)

    columns = lax.all_gather(panel[0], ("z", "core"), axis=1, tiled=True)

    def solve_first(rows):
        ready, _ = lax.optimization_barrier((inverse, moved_cols))
        return jnp.dot(rows, ready, preferred_element_type=jnp.float32).astype(
            jnp.bfloat16
        )

    def solve(rows):
        return jnp.dot(rows, inverse, preferred_element_type=jnp.float32).astype(
            jnp.bfloat16
        )

    local_trailing = trailing[0]
    rows_here = local_trailing.shape[0]
    cols_here = local_trailing.shape[1]
    share = rows_here // ncol
    block_map = extend_map[0]
    nblocks = block_map.shape[0]
    per_class = nblocks // group
    width = rows_here // (ncol * per_class)
    slots_row = jnp.arange(ncol * per_class, dtype=jnp.int32)
    class_row = slots_row // per_class
    depth_row = slots_row % per_class
    source_row = (depth_row * ncol + class_row) * nrow + row_index
    target_row = class_row * per_class + block_map[source_row] // group
    gather_row = inverse_order(target_row)
    slots_col = jnp.arange(nrow * per_class, dtype=jnp.int32)
    class_col = slots_col // per_class
    depth_col = slots_col % per_class
    source_col = (depth_col * ncol + col_index) * nrow + class_col
    target_col = class_col * per_class + block_map[source_col] // group
    gather_col = inverse_order(target_col)

    blocks_col = slots_col[:, None] == gather_col[None, :]
    same = jnp.arange(width)[:, None] == jnp.arange(width)[None, :]
    select_cols = (blocks_col[:, None, :, None] & same[None, :, None, :]).reshape(
        cols_here, cols_here
    ).astype(jnp.float32)
    moved_cols = jnp.dot(
        local_trailing,
        select_cols,
        precision=lax.Precision.HIGHEST,
        preferred_element_type=jnp.float32,
    )
    piece = solve_first(lax.dynamic_slice_in_dim(columns, col_index * share, share, 0))
    col_side = ring_gather(piece, "row", row_index, nrow)

    col_side = col_side.reshape(nrow * per_class, width, order)[gather_col].reshape(
        cols_here, order
    )

    member = lax.axis_index("front") % 2
    half = rows_here // 2
    half_blocks = half // width

    def half_update(which):
        rows = lax.dynamic_slice_in_dim(moved_cols, which * half, half, 0)
        low = solve(lax.dynamic_slice_in_dim(columns, which * half, half, 0))
        rows, low = lax.optimization_barrier((rows, low))
        schur = rows - outer_rows(low, col_side)
        blocks = (
            lax.dynamic_slice_in_dim(gather_row, which * half_blocks, half_blocks, 0)
            - which * half_blocks
        )
        return schur.reshape(half_blocks, width, cols_here)[blocks].reshape(
            half, cols_here
        )

    outgoing = half_update(1 - member).astype(jnp.bfloat16)
    incoming = from_partner(outgoing, "front", 0)
    keep = half_update(member)
    return (keep + incoming.astype(jnp.float32))[None]


def solution(mesh):
    devices = mesh.devices
    shape = devices.shape
    fine = Mesh(
        devices.reshape(shape[0], shape[1], shape[2] // 2, 2),
        ("front", "row", "z", "core"),
    )
    cols = ("z", "core")
    return jax.shard_map(
        local,
        mesh=fine,
        in_specs=(
            P("front", ("row",) + cols, None),
            P("front", "row", cols),
            P("front", "row", cols),
            P("front", None),
        ),
        out_specs=P("front", "row", cols),
        check_vma=False,
    )
```

```python
import jax
import jax.numpy as jnp
from jax import lax
from jax.sharding import Mesh
from jax.sharding import PartitionSpec as P


def from_partner(value, axis, distance):
    mask = 2**distance
    pairs = [(source, source ^ mask) for source in range(lax.axis_size(axis))]
    return lax.ppermute(value, axis, pairs)


def outer_rows(left, right):
    return lax.dot_general(
        left, right, (((1,), (1,)), ((), ())), preferred_element_type=jnp.float32
    )


def ring_gather(value, axis, index, n):
    ahead = [(source, (source + 1) % n) for source in range(n)]
    behind = [(source, (source - 1) % n) for source in range(n)]
    held = [value]
    forward = value
    backward = value
    for step in range(1, n):
        if step % 2:
            forward = lax.ppermute(forward, axis, ahead)
            held.append(forward)
        else:
            backward = lax.ppermute(backward, axis, behind)
            held.append(backward)
    offsets = [0] + [(step + 1) // 2 if step % 2 else -(step // 2) for step in range(1, n)]
    by_offset = [None] * n
    for offset, block in zip(offsets, held):
        by_offset[offset % n] = block
    stacked = jnp.stack(by_offset)
    sources = jnp.arange(n, dtype=jnp.int32)
    return stacked[(index - sources) % n]


def direct_gather(value, axis, index, n):
    held = [value]
    for offset in range(1, n):
        pairs = [(source, (source + offset) % n) for source in range(n)]
        held.append(lax.ppermute(value, axis, pairs))
    stacked = jnp.stack(held)
    sources = jnp.arange(n, dtype=jnp.int32)
    return stacked[(index - sources) % n]


def local(inverse_factor, panel, trailing, extend_map):
    nrow = lax.axis_size("row")
    nz = lax.axis_size("z")
    ncore = lax.axis_size("core")
    ncol = nz * ncore
    group = nrow * ncol
    row_index = lax.axis_index("row")
    col_index = lax.axis_index("z") * ncore + lax.axis_index("core")

    inverse = lax.all_gather(inverse_factor[0], "core", axis=0, tiled=True)
    inverse = lax.all_gather(inverse, "z", axis=0, tiled=True)
    inverse = ring_gather(inverse, "row", row_index, nrow)
    order = inverse.shape[-1]
    inverse = inverse.reshape(order, order)

    columns = lax.all_gather(panel[0], ("z", "core"), axis=1, tiled=True)

    def solve(rows):
        return jnp.dot(rows, inverse, preferred_element_type=jnp.float32).astype(
            jnp.bfloat16
        )

    local_trailing = trailing[0]
    rows_here = local_trailing.shape[0]
    cols_here = local_trailing.shape[1]
    share = rows_here // ncol
    piece = solve(lax.dynamic_slice_in_dim(columns, col_index * share, share, 0))
    col_side = direct_gather(piece, "row", row_index, nrow)

    block_map = extend_map[0]
    nblocks = block_map.shape[0]
    per_class = nblocks // group
    width = rows_here // (ncol * per_class)
    slots_row = jnp.arange(ncol * per_class, dtype=jnp.int32)
    class_row = slots_row // per_class
    depth_row = slots_row % per_class
    source_row = (depth_row * ncol + class_row) * nrow + row_index
    target_row = class_row * per_class + block_map[source_row] // group
    gather_row = jnp.argsort(target_row)
    slots_col = jnp.arange(nrow * per_class, dtype=jnp.int32)
    class_col = slots_col // per_class
    depth_col = slots_col % per_class
    source_col = (depth_col * ncol + col_index) * nrow + class_col
    target_col = class_col * per_class + block_map[source_col] // group
    gather_col = jnp.argsort(target_col)

    col_side = col_side.reshape(nrow * per_class, width, order)[gather_col].reshape(
        cols_here, order
    )
    lane = jnp.arange(cols_here, dtype=jnp.int32)
    picked = gather_col[lane // width] * width + lane % width
    select_cols = (lane[:, None] == picked[None, :]).astype(jnp.float32)

    member = lax.axis_index("front") % 2
    half = rows_here // 2
    half_blocks = half // width

    def half_update(which):
        rows = lax.dynamic_slice_in_dim(local_trailing, which * half, half, 0)
        low = solve(lax.dynamic_slice_in_dim(columns, which * half, half, 0))
        rows, low = lax.optimization_barrier((rows, low))
        moved_cols = jnp.dot(
            rows,
            select_cols,
            precision=lax.Precision.HIGHEST,
            preferred_element_type=jnp.float32,
        )
        schur = moved_cols - outer_rows(low, col_side)
        blocks = (
            lax.dynamic_slice_in_dim(gather_row, which * half_blocks, half_blocks, 0)
            - which * half_blocks
        )
        return schur.reshape(half_blocks, width, cols_here)[blocks].reshape(
            half, cols_here
        )

    outgoing = half_update(1 - member).astype(jnp.bfloat16)
    incoming = from_partner(outgoing, "front", 0)
    keep = half_update(member)
    return (keep + incoming.astype(jnp.float32))[None]


def solution(mesh):
    devices = mesh.devices
    shape = devices.shape
    fine = Mesh(
        devices.reshape(shape[0], shape[1], shape[2] // 2, 2),
        ("front", "row", "z", "core"),
    )
    cols = ("z", "core")
    return jax.shard_map(
        local,
        mesh=fine,
        in_specs=(
            P("front", ("row",) + cols, None),
            P("front", "row", cols),
            P("front", "row", cols),
            P("front", None),
        ),
        out_specs=P("front", "row", cols),
        check_vma=False,
    )
```

```python
import jax
import jax.numpy as jnp
from jax import lax
from jax.sharding import Mesh
from jax.sharding import PartitionSpec as P


def from_partner(value, axis, distance):
    mask = 2**distance
    pairs = [(source, source ^ mask) for source in range(lax.axis_size(axis))]
    return lax.ppermute(value, axis, pairs)


def outer_rows(left, right):
    return lax.dot_general(
        left, right, (((1,), (1,)), ((), ())), preferred_element_type=jnp.float32
    )


def ring_gather(value, axis, index, n):
    ahead = [(source, (source + 1) % n) for source in range(n)]
    behind = [(source, (source - 1) % n) for source in range(n)]
    held = [value]
    forward = value
    backward = value
    for step in range(1, n):
        if step % 2:
            forward = lax.ppermute(forward, axis, ahead)
            held.append(forward)
        else:
            backward = lax.ppermute(backward, axis, behind)
            held.append(backward)
    offsets = [0] + [(step + 1) // 2 if step % 2 else -(step // 2) for step in range(1, n)]
    by_offset = [None] * n
    for offset, block in zip(offsets, held):
        by_offset[offset % n] = block
    stacked = jnp.stack(by_offset)
    sources = jnp.arange(n, dtype=jnp.int32)
    return stacked[(index - sources) % n]


def direct_gather(value, axis, index, n):
    held = [value]
    for offset in range(1, n):
        pairs = [(source, (source + offset) % n) for source in range(n)]
        held.append(lax.ppermute(value, axis, pairs))
    stacked = jnp.stack(held)
    sources = jnp.arange(n, dtype=jnp.int32)
    return stacked[(index - sources) % n]


def local(inverse_factor, panel, trailing, extend_map):
    nrow = lax.axis_size("row")
    nz = lax.axis_size("z")
    ncore = lax.axis_size("core")
    ncol = nz * ncore
    group = nrow * ncol
    row_index = lax.axis_index("row")
    col_index = lax.axis_index("z") * ncore + lax.axis_index("core")

    inverse = lax.all_gather(inverse_factor[0], "core", axis=0, tiled=True)
    inverse = lax.all_gather(inverse, "z", axis=0, tiled=True)
    inverse = ring_gather(inverse, "row", row_index, nrow)
    order = inverse.shape[-1]
    inverse = inverse.reshape(order, order)

    columns = lax.all_gather(panel[0], ("z", "core"), axis=1, tiled=True)

    def solve(rows):
        return jnp.dot(rows, inverse, preferred_element_type=jnp.float32).astype(
            jnp.bfloat16
        )

    local_trailing = trailing[0]
    rows_here = local_trailing.shape[0]
    cols_here = local_trailing.shape[1]
    share = rows_here // ncol
    piece = solve(lax.dynamic_slice_in_dim(columns, col_index * share, share, 0))
    col_side = direct_gather(piece, "row", row_index, nrow)

    block_map = extend_map[0]
    nblocks = block_map.shape[0]
    per_class = nblocks // group
    width = rows_here // (ncol * per_class)
    slots_row = jnp.arange(ncol * per_class, dtype=jnp.int32)
    class_row = slots_row // per_class
    depth_row = slots_row % per_class
    source_row = (depth_row * ncol + class_row) * nrow + row_index
    target_row = class_row * per_class + block_map[source_row] // group
    gather_row = jnp.argsort(target_row)
    slots_col = jnp.arange(nrow * per_class, dtype=jnp.int32)
    class_col = slots_col // per_class
    depth_col = slots_col % per_class
    source_col = (depth_col * ncol + col_index) * nrow + class_col
    target_col = class_col * per_class + block_map[source_col] // group
    gather_col = jnp.argsort(target_col)

    col_side = col_side.reshape(nrow * per_class, width, order)[gather_col].reshape(
        cols_here, order
    )
    lane = jnp.arange(cols_here, dtype=jnp.int32)
    picked = gather_col[lane // width] * width + lane % width
    select_cols = (lane[:, None] == picked[None, :]).astype(jnp.float32)

    member = lax.axis_index("front") % 2
    half = rows_here // 2
    half_blocks = half // width

    def half_update(which, after=None):
        rows = lax.dynamic_slice_in_dim(local_trailing, which * half, half, 0)
        own = lax.dynamic_slice_in_dim(columns, which * half, half, 0)
        if after is not None:
            own, _ = lax.optimization_barrier((own, after))
        low = solve(own)
        rows, low = lax.optimization_barrier((rows, low))
        moved_cols = jnp.dot(
            rows,
            select_cols,
            precision=lax.Precision.HIGHEST,
            preferred_element_type=jnp.float32,
        )
        schur = moved_cols - outer_rows(low, col_side)
        blocks = (
            lax.dynamic_slice_in_dim(gather_row, which * half_blocks, half_blocks, 0)
            - which * half_blocks
        )
        return schur.reshape(half_blocks, width, cols_here)[blocks].reshape(
            half, cols_here
        )

    outgoing = half_update(1 - member).astype(jnp.bfloat16)
    incoming = from_partner(outgoing, "front", 0)
    keep = half_update(member, outgoing)
    return (keep + incoming.astype(jnp.float32))[None]


def solution(mesh):
    devices = mesh.devices
    shape = devices.shape
    fine = Mesh(
        devices.reshape(shape[0], shape[1], shape[2] // 2, 2),
        ("front", "row", "z", "core"),
    )
    cols = ("z", "core")
    return jax.shard_map(
        local,
        mesh=fine,
        in_specs=(
            P("front", ("row",) + cols, None),
            P("front", "row", cols),
            P("front", "row", cols),
            P("front", None),
        ),
        out_specs=P("front", "row", cols),
        check_vma=False,
    )
```

```python
import jax
import jax.numpy as jnp
from jax import lax
from jax.sharding import Mesh
from jax.sharding import PartitionSpec as P


def from_partner(value, axis, distance):
    mask = 2**distance
    pairs = [(source, source ^ mask) for source in range(lax.axis_size(axis))]
    return lax.ppermute(value, axis, pairs)


def outer_rows(left, right):
    return lax.dot_general(
        left, right, (((1,), (1,)), ((), ())), preferred_element_type=jnp.float32
    )


def ring_gather(value, axis, index, n):
    ahead = [(source, (source + 1) % n) for source in range(n)]
    behind = [(source, (source - 1) % n) for source in range(n)]
    held = [value]
    forward = value
    backward = value
    for step in range(1, n):
        if step % 2:
            forward = lax.ppermute(forward, axis, ahead)
            held.append(forward)
        else:
            backward = lax.ppermute(backward, axis, behind)
            held.append(backward)
    offsets = [0] + [(step + 1) // 2 if step % 2 else -(step // 2) for step in range(1, n)]
    by_offset = [None] * n
    for offset, block in zip(offsets, held):
        by_offset[offset % n] = block
    stacked = jnp.stack(by_offset)
    sources = jnp.arange(n, dtype=jnp.int32)
    return stacked[(index - sources) % n]


def local(inverse_factor, panel, trailing, extend_map):
    nrow = lax.axis_size("row")
    nz = lax.axis_size("z")
    ncore = lax.axis_size("core")
    ncol = nz * ncore
    group = nrow * ncol
    row_index = lax.axis_index("row")
    col_index = lax.axis_index("z") * ncore + lax.axis_index("core")

    inverse = lax.all_gather(inverse_factor[0], "core", axis=0, tiled=True)
    inverse = lax.all_gather(inverse, "z", axis=0, tiled=True)
    inverse = ring_gather(inverse, "row", row_index, nrow)
    order = inverse.shape[-1]
    inverse = inverse.reshape(order, order)

    columns = lax.all_gather(panel[0], ("z", "core"), axis=1, tiled=True)

    def solve(rows):
        return jnp.dot(rows, inverse, preferred_element_type=jnp.float32).astype(
            jnp.bfloat16
        )

    local_trailing = trailing[0]
    rows_here = local_trailing.shape[0]
    cols_here = local_trailing.shape[1]
    share = rows_here // ncol
    piece = solve(lax.dynamic_slice_in_dim(columns, col_index * share, share, 0))
    col_side = lax.all_to_all(
        jnp.broadcast_to(piece[None], (nrow,) + piece.shape), "row", 0, 0, tiled=True
    )

    block_map = extend_map[0]
    nblocks = block_map.shape[0]
    per_class = nblocks // group
    width = rows_here // (ncol * per_class)
    slots_row = jnp.arange(ncol * per_class, dtype=jnp.int32)
    class_row = slots_row // per_class
    depth_row = slots_row % per_class
    source_row = (depth_row * ncol + class_row) * nrow + row_index
    target_row = class_row * per_class + block_map[source_row] // group
    gather_row = jnp.argsort(target_row)
    slots_col = jnp.arange(nrow * per_class, dtype=jnp.int32)
    class_col = slots_col // per_class
    depth_col = slots_col % per_class
    source_col = (depth_col * ncol + col_index) * nrow + class_col
    target_col = class_col * per_class + block_map[source_col] // group
    gather_col = jnp.argsort(target_col)

    col_side = col_side.reshape(nrow * per_class, width, order)[gather_col].reshape(
        cols_here, order
    )
    lane = jnp.arange(cols_here, dtype=jnp.int32)
    picked = gather_col[lane // width] * width + lane % width
    select_cols = (lane[:, None] == picked[None, :]).astype(jnp.float32)

    member = lax.axis_index("front") % 2
    half = rows_here // 2
    half_blocks = half // width

    def half_update(which):
        rows = lax.dynamic_slice_in_dim(local_trailing, which * half, half, 0)
        low = solve(lax.dynamic_slice_in_dim(columns, which * half, half, 0))
        rows, low = lax.optimization_barrier((rows, low))
        moved_cols = jnp.dot(
            rows,
            select_cols,
            precision=lax.Precision.HIGHEST,
            preferred_element_type=jnp.float32,
        )
        schur = moved_cols - outer_rows(low, col_side)
        blocks = (
            lax.dynamic_slice_in_dim(gather_row, which * half_blocks, half_blocks, 0)
            - which * half_blocks
        )
        return schur.reshape(half_blocks, width, cols_here)[blocks].reshape(
            half, cols_here
        )

    outgoing = half_update(1 - member).astype(jnp.bfloat16)
    incoming = from_partner(outgoing, "front", 0)
    keep = half_update(member)
    return (keep + incoming.astype(jnp.float32))[None]


def solution(mesh):
    devices = mesh.devices
    shape = devices.shape
    fine = Mesh(
        devices.reshape(shape[0], shape[1], shape[2] // 2, 2),
        ("front", "row", "z", "core"),
    )
    cols = ("z", "core")
    return jax.shard_map(
        local,
        mesh=fine,
        in_specs=(
            P("front", ("row",) + cols, None),
            P("front", "row", cols),
            P("front", "row", cols),
            P("front", None),
        ),
        out_specs=P("front", "row", cols),
        check_vma=False,
    )
```

```python
import jax
import jax.numpy as jnp
from jax import lax
from jax.sharding import Mesh
from jax.sharding import PartitionSpec as P


def from_partner(value, axis, distance):
    mask = 2**distance
    pairs = [(source, source ^ mask) for source in range(lax.axis_size(axis))]
    return lax.ppermute(value, axis, pairs)


def outer_rows(left, right):
    return lax.dot_general(
        left, right, (((1,), (1,)), ((), ())), preferred_element_type=jnp.float32
    )


def ring_gather(value, axis, index, n):
    ahead = [(source, (source + 1) % n) for source in range(n)]
    behind = [(source, (source - 1) % n) for source in range(n)]
    held = [value]
    forward = value
    backward = value
    for step in range(1, n):
        if step % 2:
            forward = lax.ppermute(forward, axis, ahead)
            held.append(forward)
        else:
            backward = lax.ppermute(backward, axis, behind)
            held.append(backward)
    offsets = [0] + [(step + 1) // 2 if step % 2 else -(step // 2) for step in range(1, n)]
    by_offset = [None] * n
    for offset, block in zip(offsets, held):
        by_offset[offset % n] = block
    stacked = jnp.stack(by_offset)
    sources = jnp.arange(n, dtype=jnp.int32)
    return stacked[(index - sources) % n]


def local(inverse_factor, panel, trailing, extend_map):
    nrow = lax.axis_size("row")
    nz = lax.axis_size("z")
    ncore = lax.axis_size("core")
    ncol = nz * ncore
    group = nrow * ncol
    row_index = lax.axis_index("row")
    col_index = lax.axis_index("z") * ncore + lax.axis_index("core")

    inverse = lax.all_gather(inverse_factor[0], "core", axis=0, tiled=True)
    inverse = lax.all_gather(inverse, "z", axis=0, tiled=True)
    inverse = ring_gather(inverse, "row", row_index, nrow)
    order = inverse.shape[-1]
    inverse = inverse.reshape(order, order)

    columns = lax.all_gather(panel[0], ("z", "core"), axis=1, tiled=True)

    step = order // 4

    def solve(rows):
        parts = [
            jnp.dot(
                rows[:, : end + step],
                inverse[: end + step, end : end + step],
                preferred_element_type=jnp.float32,
            ).astype(jnp.bfloat16)
            for end in range(0, order, step)
        ]
        return jnp.concatenate(parts, axis=1)

    local_trailing = trailing[0]
    rows_here = local_trailing.shape[0]
    cols_here = local_trailing.shape[1]
    share = rows_here // ncol
    piece = solve(lax.dynamic_slice_in_dim(columns, col_index * share, share, 0))
    col_side = lax.all_to_all(
        jnp.broadcast_to(piece[None], (nrow,) + piece.shape), "row", 0, 0, tiled=True
    )

    block_map = extend_map[0]
    nblocks = block_map.shape[0]
    per_class = nblocks // group
    width = rows_here // (ncol * per_class)
    slots_row = jnp.arange(ncol * per_class, dtype=jnp.int32)
    class_row = slots_row // per_class
    depth_row = slots_row % per_class
    source_row = (depth_row * ncol + class_row) * nrow + row_index
    target_row = class_row * per_class + block_map[source_row] // group
    gather_row = jnp.argsort(target_row)
    slots_col = jnp.arange(nrow * per_class, dtype=jnp.int32)
    class_col = slots_col // per_class
    depth_col = slots_col % per_class
    source_col = (depth_col * ncol + col_index) * nrow + class_col
    target_col = class_col * per_class + block_map[source_col] // group
    gather_col = jnp.argsort(target_col)

    col_side = col_side.reshape(nrow * per_class, width, order)[gather_col].reshape(
        cols_here, order
    )
    lane = jnp.arange(cols_here, dtype=jnp.int32)
    picked = gather_col[lane // width] * width + lane % width
    select_cols = (lane[:, None] == picked[None, :]).astype(jnp.float32)

    member = lax.axis_index("front") % 2
    half = rows_here // 2
    half_blocks = half // width

    def half_update(which):
        rows = lax.dynamic_slice_in_dim(local_trailing, which * half, half, 0)
        low = solve(lax.dynamic_slice_in_dim(columns, which * half, half, 0))
        rows, low = lax.optimization_barrier((rows, low))
        moved_cols = jnp.dot(
            rows,
            select_cols,
            precision=lax.Precision.HIGHEST,
            preferred_element_type=jnp.float32,
        )
        schur = moved_cols - outer_rows(low, col_side)
        blocks = (
            lax.dynamic_slice_in_dim(gather_row, which * half_blocks, half_blocks, 0)
            - which * half_blocks
        )
        return schur.reshape(half_blocks, width, cols_here)[blocks].reshape(
            half, cols_here
        )

    outgoing = half_update(1 - member).astype(jnp.bfloat16)
    incoming = from_partner(outgoing, "front", 0)
    keep = half_update(member)
    return (keep + incoming.astype(jnp.float32))[None]


def solution(mesh):
    devices = mesh.devices
    shape = devices.shape
    fine = Mesh(
        devices.reshape(shape[0], shape[1], shape[2] // 2, 2),
        ("front", "row", "z", "core"),
    )
    cols = ("z", "core")
    return jax.shard_map(
        local,
        mesh=fine,
        in_specs=(
            P("front", ("row",) + cols, None),
            P("front", "row", cols),
            P("front", "row", cols),
            P("front", None),
        ),
        out_specs=P("front", "row", cols),
        check_vma=False,
    )
```

```python
import jax
import jax.numpy as jnp
from jax import lax
from jax.sharding import Mesh
from jax.sharding import PartitionSpec as P


def from_partner(value, axis, distance):
    mask = 2**distance
    pairs = [(source, source ^ mask) for source in range(lax.axis_size(axis))]
    return lax.ppermute(value, axis, pairs)


def outer_rows(left, right):
    return lax.dot_general(
        left, right, (((1,), (1,)), ((), ())), preferred_element_type=jnp.float32
    )


def ring_gather(value, axis, index, n):
    ahead = [(source, (source + 1) % n) for source in range(n)]
    behind = [(source, (source - 1) % n) for source in range(n)]
    held = [value]
    forward = value
    backward = value
    for step in range(1, n):
        if step % 2:
            forward = lax.ppermute(forward, axis, ahead)
            held.append(forward)
        else:
            backward = lax.ppermute(backward, axis, behind)
            held.append(backward)
    offsets = [0] + [(step + 1) // 2 if step % 2 else -(step // 2) for step in range(1, n)]
    by_offset = [None] * n
    for offset, block in zip(offsets, held):
        by_offset[offset % n] = block
    stacked = jnp.stack(by_offset)
    sources = jnp.arange(n, dtype=jnp.int32)
    return stacked[(index - sources) % n]


def local(inverse_factor, panel, trailing, extend_map):
    nrow = lax.axis_size("row")
    nz = lax.axis_size("z")
    ncore = lax.axis_size("core")
    ncol = nz * ncore
    group = nrow * ncol
    row_index = lax.axis_index("row")
    col_index = lax.axis_index("z") * ncore + lax.axis_index("core")

    inverse = lax.all_gather(inverse_factor[0], "core", axis=0, tiled=True)
    inverse = lax.all_gather(inverse, "z", axis=0, tiled=True)
    inverse = ring_gather(inverse, "row", row_index, nrow)
    order = inverse.shape[-1]
    inverse = inverse.reshape(order, order)

    columns = lax.all_gather(panel[0], ("z", "core"), axis=1, tiled=True)

    def solve(rows):
        return jnp.dot(rows, inverse, preferred_element_type=jnp.float32).astype(
            jnp.bfloat16
        )

    local_trailing = trailing[0]
    rows_here = local_trailing.shape[0]
    cols_here = local_trailing.shape[1]
    share = rows_here // ncol
    piece = solve(lax.dynamic_slice_in_dim(columns, col_index * share, share, 0))

    block_map = extend_map[0]
    nblocks = block_map.shape[0]
    per_class = nblocks // group
    width = rows_here // (ncol * per_class)
    slots_row = jnp.arange(ncol * per_class, dtype=jnp.int32)
    class_row = slots_row // per_class
    depth_row = slots_row % per_class
    source_row = (depth_row * ncol + class_row) * nrow + row_index
    target_row = class_row * per_class + block_map[source_row] // group
    gather_row = jnp.argsort(target_row)
    slots_col = jnp.arange(nrow * per_class, dtype=jnp.int32)
    class_col = slots_col // per_class
    depth_col = slots_col % per_class
    source_col = (depth_col * ncol + col_index) * nrow + class_col
    target_col = class_col * per_class + block_map[source_col] // group
    gather_col = jnp.argsort(target_col)

    own_blocks = (
        lax.dynamic_slice_in_dim(gather_col, row_index * per_class, per_class, 0)
        - row_index * per_class
    )
    piece = piece.reshape(per_class, width, order)[own_blocks].reshape(share, order)
    col_side = lax.all_to_all(
        jnp.broadcast_to(piece[None], (nrow,) + piece.shape), "row", 0, 0, tiled=True
    ).reshape(cols_here, order)
    lane = jnp.arange(cols_here, dtype=jnp.int32)
    picked = gather_col[lane // width] * width + lane % width
    select_cols = (lane[:, None] == picked[None, :]).astype(jnp.float32)

    member = lax.axis_index("front") % 2
    half = rows_here // 2
    half_blocks = half // width

    def half_update(which):
        rows = lax.dynamic_slice_in_dim(local_trailing, which * half, half, 0)
        low = solve(lax.dynamic_slice_in_dim(columns, which * half, half, 0))
        rows, low = lax.optimization_barrier((rows, low))
        moved_cols = jnp.dot(
            rows,
            select_cols,
            precision=lax.Precision.HIGHEST,
            preferred_element_type=jnp.float32,
        )
        schur = moved_cols - outer_rows(low, col_side)
        blocks = (
            lax.dynamic_slice_in_dim(gather_row, which * half_blocks, half_blocks, 0)
            - which * half_blocks
        )
        return schur.reshape(half_blocks, width, cols_here)[blocks].reshape(
            half, cols_here
        )

    outgoing = half_update(1 - member).astype(jnp.bfloat16)
    incoming = from_partner(outgoing, "front", 0)
    keep = half_update(member)
    return (keep + incoming.astype(jnp.float32))[None]


def solution(mesh):
    devices = mesh.devices
    shape = devices.shape
    fine = Mesh(
        devices.reshape(shape[0], shape[1], shape[2] // 2, 2),
        ("front", "row", "z", "core"),
    )
    cols = ("z", "core")
    return jax.shard_map(
        local,
        mesh=fine,
        in_specs=(
            P("front", ("row",) + cols, None),
            P("front", "row", cols),
            P("front", "row", cols),
            P("front", None),
        ),
        out_specs=P("front", "row", cols),
        check_vma=False,
    )
```

```python
import jax
import jax.numpy as jnp
from jax import lax
from jax.sharding import Mesh
from jax.sharding import PartitionSpec as P


def from_partner(value, axis, distance):
    mask = 2**distance
    pairs = [(source, source ^ mask) for source in range(lax.axis_size(axis))]
    return lax.ppermute(value, axis, pairs)


def outer_rows(left, right):
    return lax.dot_general(
        left, right, (((1,), (1,)), ((), ())), preferred_element_type=jnp.float32
    )


def ring_gather(value, axis, index, n):
    ahead = [(source, (source + 1) % n) for source in range(n)]
    behind = [(source, (source - 1) % n) for source in range(n)]
    held = [value]
    forward = value
    backward = value
    for step in range(1, n):
        if step % 2:
            forward = lax.ppermute(forward, axis, ahead)
            held.append(forward)
        else:
            backward = lax.ppermute(backward, axis, behind)
            held.append(backward)
    offsets = [0] + [(step + 1) // 2 if step % 2 else -(step // 2) for step in range(1, n)]
    by_offset = [None] * n
    for offset, block in zip(offsets, held):
        by_offset[offset % n] = block
    stacked = jnp.stack(by_offset)
    sources = jnp.arange(n, dtype=jnp.int32)
    return stacked[(index - sources) % n]


def local(inverse_factor, panel, trailing, extend_map):
    nrow = lax.axis_size("row")
    nz = lax.axis_size("z")
    ncore = lax.axis_size("core")
    ncol = nz * ncore
    group = nrow * ncol
    row_index = lax.axis_index("row")
    col_index = lax.axis_index("z") * ncore + lax.axis_index("core")

    inverse = lax.all_gather(inverse_factor[0], "core", axis=0, tiled=True)
    inverse = lax.all_gather(inverse, "z", axis=0, tiled=True)
    inverse = ring_gather(inverse, "row", row_index, nrow)
    order = inverse.shape[-1]
    inverse = inverse.reshape(order, order)

    columns = lax.all_gather(panel[0], ("z", "core"), axis=1, tiled=True)

    def solve(rows):
        return jnp.dot(rows, inverse, preferred_element_type=jnp.float32).astype(
            jnp.bfloat16
        )

    local_trailing = trailing[0]
    rows_here = local_trailing.shape[0]
    cols_here = local_trailing.shape[1]
    share = rows_here // ncol
    piece = solve(lax.dynamic_slice_in_dim(columns, col_index * share, share, 0))

    block_map = extend_map[0]
    nblocks = block_map.shape[0]
    per_class = nblocks // group
    width = rows_here // (ncol * per_class)
    slots_row = jnp.arange(ncol * per_class, dtype=jnp.int32)
    class_row = slots_row // per_class
    depth_row = slots_row % per_class
    source_row = (depth_row * ncol + class_row) * nrow + row_index
    target_row = class_row * per_class + block_map[source_row] // group
    gather_row = jnp.argsort(target_row)
    slots_col = jnp.arange(nrow * per_class, dtype=jnp.int32)
    class_col = slots_col // per_class
    depth_col = slots_col % per_class
    source_col = (depth_col * ncol + col_index) * nrow + class_col
    target_col = class_col * per_class + block_map[source_col] // group
    gather_col = jnp.argsort(target_col)

    own_blocks = (
        lax.dynamic_slice_in_dim(gather_col, row_index * per_class, per_class, 0)
        - row_index * per_class
    )
    piece = piece.reshape(per_class, width, order)[own_blocks].reshape(share, order)
    col_side = lax.all_to_all(
        jnp.broadcast_to(piece[None], (nrow,) + piece.shape), "row", 0, 0, tiled=True
    ).reshape(cols_here, order)
    lane = jnp.arange(cols_here, dtype=jnp.int32)
    picked = gather_col[lane // width] * width + lane % width
    select_cols = (lane[:, None] == picked[None, :]).astype(jnp.float32)

    member = lax.axis_index("front") % 2
    half = rows_here // 2
    half_blocks = half // width

    def half_update(which, after=None):
        rows = lax.dynamic_slice_in_dim(local_trailing, which * half, half, 0)
        own = lax.dynamic_slice_in_dim(columns, which * half, half, 0)
        if after is not None:
            own, _ = lax.optimization_barrier((own, after))
        low = solve(own)
        rows, low = lax.optimization_barrier((rows, low))
        moved_cols = jnp.dot(
            rows,
            select_cols,
            precision=lax.Precision.HIGHEST,
            preferred_element_type=jnp.float32,
        )
        schur = moved_cols - outer_rows(low, col_side)
        blocks = (
            lax.dynamic_slice_in_dim(gather_row, which * half_blocks, half_blocks, 0)
            - which * half_blocks
        )
        return schur.reshape(half_blocks, width, cols_here)[blocks].reshape(
            half, cols_here
        )

    outgoing = half_update(1 - member).astype(jnp.bfloat16)
    incoming = from_partner(outgoing, "front", 0)
    keep = half_update(member, outgoing)
    return (keep + incoming.astype(jnp.float32))[None]


def solution(mesh):
    devices = mesh.devices
    shape = devices.shape
    fine = Mesh(
        devices.reshape(shape[0], shape[1], shape[2] // 2, 2),
        ("front", "row", "z", "core"),
    )
    cols = ("z", "core")
    return jax.shard_map(
        local,
        mesh=fine,
        in_specs=(
            P("front", ("row",) + cols, None),
            P("front", "row", cols),
            P("front", "row", cols),
            P("front", None),
        ),
        out_specs=P("front", "row", cols),
        check_vma=False,
    )
```

```python
import jax
import jax.numpy as jnp
from jax import lax
from jax.sharding import Mesh
from jax.sharding import PartitionSpec as P


def from_partner(value, axis, distance):
    mask = 2**distance
    pairs = [(source, source ^ mask) for source in range(lax.axis_size(axis))]
    return lax.ppermute(value, axis, pairs)


def outer_rows(left, right):
    return lax.dot_general(
        left, right, (((1,), (1,)), ((), ())), preferred_element_type=jnp.float32
    )


def ring_gather(value, axis, index, n):
    ahead = [(source, (source + 1) % n) for source in range(n)]
    behind = [(source, (source - 1) % n) for source in range(n)]
    held = [value]
    forward = value
    backward = value
    for step in range(1, n):
        if step % 2:
            forward = lax.ppermute(forward, axis, ahead)
            held.append(forward)
        else:
            backward = lax.ppermute(backward, axis, behind)
            held.append(backward)
    offsets = [0] + [(step + 1) // 2 if step % 2 else -(step // 2) for step in range(1, n)]
    by_offset = [None] * n
    for offset, block in zip(offsets, held):
        by_offset[offset % n] = block
    stacked = jnp.stack(by_offset)
    sources = jnp.arange(n, dtype=jnp.int32)
    return stacked[(index - sources) % n]


def local(inverse_factor, panel, trailing, extend_map):
    nrow = lax.axis_size("row")
    nz = lax.axis_size("z")
    ncore = lax.axis_size("core")
    ncol = nz * ncore
    group = nrow * ncol
    row_index = lax.axis_index("row")
    col_index = lax.axis_index("z") * ncore + lax.axis_index("core")

    inverse = lax.all_gather(inverse_factor[0], "core", axis=0, tiled=True)
    inverse = lax.all_gather(inverse, "z", axis=0, tiled=True)
    inverse = ring_gather(inverse, "row", row_index, nrow)
    order = inverse.shape[-1]
    inverse = inverse.reshape(order, order)

    columns = lax.all_gather(panel[0], ("z", "core"), axis=1, tiled=True)

    def solve(rows):
        return jnp.dot(rows, inverse, preferred_element_type=jnp.float32).astype(
            jnp.bfloat16
        )

    local_trailing = trailing[0]
    rows_here = local_trailing.shape[0]
    cols_here = local_trailing.shape[1]
    share = rows_here // ncol
    piece = solve(lax.dynamic_slice_in_dim(columns, col_index * share, share, 0))

    block_map = extend_map[0]
    nblocks = block_map.shape[0]
    per_class = nblocks // group
    width = rows_here // (ncol * per_class)
    slots_row = jnp.arange(ncol * per_class, dtype=jnp.int32)
    class_row = slots_row // per_class
    depth_row = slots_row % per_class
    source_row = (depth_row * ncol + class_row) * nrow + row_index
    target_row = class_row * per_class + block_map[source_row] // group
    gather_row = jnp.argsort(target_row)
    slots_col = jnp.arange(nrow * per_class, dtype=jnp.int32)
    class_col = slots_col // per_class
    depth_col = slots_col % per_class
    source_col = (depth_col * ncol + col_index) * nrow + class_col
    target_col = class_col * per_class + block_map[source_col] // group
    gather_col = jnp.argsort(target_col)

    own_blocks = (
        lax.dynamic_slice_in_dim(gather_col, row_index * per_class, per_class, 0)
        - row_index * per_class
    )
    piece = piece.reshape(per_class, width, order)[own_blocks].reshape(share, order)
    col_side = lax.all_to_all(
        jnp.broadcast_to(piece[None], (nrow,) + piece.shape), "row", 0, 0, tiled=True
    ).reshape(cols_here, order)
    lane = jnp.arange(cols_here, dtype=jnp.int32)
    picked = gather_col[lane // width] * width + lane % width
    select_cols = (lane[:, None] == picked[None, :]).astype(jnp.float32)

    solved = solve(columns)
    member = lax.axis_index("front") % 2
    half = rows_here // 2
    half_blocks = half // width

    def half_update(which):
        rows = lax.dynamic_slice_in_dim(local_trailing, which * half, half, 0)
        low = lax.dynamic_slice_in_dim(solved, which * half, half, 0)
        rows, low = lax.optimization_barrier((rows, low))
        moved_cols = jnp.dot(
            rows,
            select_cols,
            precision=lax.Precision.HIGHEST,
            preferred_element_type=jnp.float32,
        )
        schur = moved_cols - outer_rows(low, col_side)
        blocks = (
            lax.dynamic_slice_in_dim(gather_row, which * half_blocks, half_blocks, 0)
            - which * half_blocks
        )
        return schur.reshape(half_blocks, width, cols_here)[blocks].reshape(
            half, cols_here
        )

    outgoing = half_update(1 - member).astype(jnp.bfloat16)
    incoming = from_partner(outgoing, "front", 0)
    keep = half_update(member)
    return (keep + incoming.astype(jnp.float32))[None]


def solution(mesh):
    devices = mesh.devices
    shape = devices.shape
    fine = Mesh(
        devices.reshape(shape[0], shape[1], shape[2] // 2, 2),
        ("front", "row", "z", "core"),
    )
    cols = ("z", "core")
    return jax.shard_map(
        local,
        mesh=fine,
        in_specs=(
            P("front", ("row",) + cols, None),
            P("front", "row", cols),
            P("front", "row", cols),
            P("front", None),
        ),
        out_specs=P("front", "row", cols),
        check_vma=False,
    )
```

```python
import jax
import jax.numpy as jnp
from jax import lax
from jax.sharding import Mesh
from jax.sharding import PartitionSpec as P


def from_partner(value, axis, distance):
    mask = 2**distance
    pairs = [(source, source ^ mask) for source in range(lax.axis_size(axis))]
    return lax.ppermute(value, axis, pairs)


def outer_rows(left, right):
    return lax.dot_general(
        left, right, (((1,), (1,)), ((), ())), preferred_element_type=jnp.float32
    )


def ring_gather(value, axis, index, n):
    ahead = [(source, (source + 1) % n) for source in range(n)]
    behind = [(source, (source - 1) % n) for source in range(n)]
    held = [value]
    forward = value
    backward = value
    for step in range(1, n):
        if step % 2:
            forward = lax.ppermute(forward, axis, ahead)
            held.append(forward)
        else:
            backward = lax.ppermute(backward, axis, behind)
            held.append(backward)
    offsets = [0] + [(step + 1) // 2 if step % 2 else -(step // 2) for step in range(1, n)]
    by_offset = [None] * n
    for offset, block in zip(offsets, held):
        by_offset[offset % n] = block
    stacked = jnp.stack(by_offset)
    sources = jnp.arange(n, dtype=jnp.int32)
    return stacked[(index - sources) % n]


def local(inverse_factor, panel, trailing, extend_map):
    nrow = lax.axis_size("row")
    nz = lax.axis_size("z")
    ncore = lax.axis_size("core")
    ncol = nz * ncore
    group = nrow * ncol
    row_index = lax.axis_index("row")
    col_index = lax.axis_index("z") * ncore + lax.axis_index("core")

    inverse = lax.all_gather(inverse_factor[0], "core", axis=0, tiled=True)
    inverse = lax.all_gather(inverse, "z", axis=0, tiled=True)
    inverse = ring_gather(inverse, "row", row_index, nrow)
    order = inverse.shape[-1]
    inverse = inverse.reshape(order, order)

    columns = lax.all_gather(panel[0], ("z", "core"), axis=1, tiled=True)

    def solve(rows):
        return jnp.dot(rows, inverse, preferred_element_type=jnp.float32).astype(
            jnp.bfloat16
        )

    local_trailing = trailing[0]
    rows_here = local_trailing.shape[0]
    cols_here = local_trailing.shape[1]
    share = rows_here // ncol
    piece = solve(lax.dynamic_slice_in_dim(columns, col_index * share, share, 0))

    block_map = extend_map[0]
    nblocks = block_map.shape[0]
    per_class = nblocks // group
    width = rows_here // (ncol * per_class)
    slots_row = jnp.arange(ncol * per_class, dtype=jnp.int32)
    class_row = slots_row // per_class
    depth_row = slots_row % per_class
    source_row = (depth_row * ncol + class_row) * nrow + row_index
    target_row = class_row * per_class + block_map[source_row] // group
    gather_row = jnp.argsort(target_row)
    slots_col = jnp.arange(nrow * per_class, dtype=jnp.int32)
    class_col = slots_col // per_class
    depth_col = slots_col % per_class
    source_col = (depth_col * ncol + col_index) * nrow + class_col
    target_col = class_col * per_class + block_map[source_col] // group
    gather_col = jnp.argsort(target_col)

    own_blocks = (
        lax.dynamic_slice_in_dim(gather_col, row_index * per_class, per_class, 0)
        - row_index * per_class
    )
    copies = jnp.tile(own_blocks, nrow)
    piece = piece.reshape(per_class, width, order)[copies].reshape(nrow, share, order)
    col_side = lax.all_to_all(piece, "row", 0, 0, tiled=True).reshape(cols_here, order)
    lane = jnp.arange(cols_here, dtype=jnp.int32)
    picked = gather_col[lane // width] * width + lane % width
    select_cols = (lane[:, None] == picked[None, :]).astype(jnp.float32)

    solved = solve(columns)
    member = lax.axis_index("front") % 2
    half = rows_here // 2
    half_blocks = half // width

    def half_update(which):
        rows = lax.dynamic_slice_in_dim(local_trailing, which * half, half, 0)
        low = lax.dynamic_slice_in_dim(solved, which * half, half, 0)
        rows, low = lax.optimization_barrier((rows, low))
        moved_cols = jnp.dot(
            rows,
            select_cols,
            precision=lax.Precision.HIGHEST,
            preferred_element_type=jnp.float32,
        )
        schur = moved_cols - outer_rows(low, col_side)
        blocks = (
            lax.dynamic_slice_in_dim(gather_row, which * half_blocks, half_blocks, 0)
            - which * half_blocks
        )
        return schur.reshape(half_blocks, width, cols_here)[blocks].reshape(
            half, cols_here
        )

    outgoing = half_update(1 - member).astype(jnp.bfloat16)
    incoming = from_partner(outgoing, "front", 0)
    keep = half_update(member)
    return (keep + incoming.astype(jnp.float32))[None]


def solution(mesh):
    devices = mesh.devices
    shape = devices.shape
    fine = Mesh(
        devices.reshape(shape[0], shape[1], shape[2] // 2, 2),
        ("front", "row", "z", "core"),
    )
    cols = ("z", "core")
    return jax.shard_map(
        local,
        mesh=fine,
        in_specs=(
            P("front", ("row",) + cols, None),
            P("front", "row", cols),
            P("front", "row", cols),
            P("front", None),
        ),
        out_specs=P("front", "row", cols),
        check_vma=False,
    )
```

```python
import jax
import jax.numpy as jnp
from jax import lax
from jax.sharding import Mesh
from jax.sharding import PartitionSpec as P


def from_partner(value, axis, distance):
    mask = 2**distance
    pairs = [(source, source ^ mask) for source in range(lax.axis_size(axis))]
    return lax.ppermute(value, axis, pairs)


def outer_rows(left, right):
    return lax.dot_general(
        left, right, (((1,), (1,)), ((), ())), preferred_element_type=jnp.float32
    )


def ring_gather(value, axis, index, n):
    ahead = [(source, (source + 1) % n) for source in range(n)]
    behind = [(source, (source - 1) % n) for source in range(n)]
    held = [value]
    forward = value
    backward = value
    for step in range(1, n):
        if step % 2:
            forward = lax.ppermute(forward, axis, ahead)
            held.append(forward)
        else:
            backward = lax.ppermute(backward, axis, behind)
            held.append(backward)
    offsets = [0] + [(step + 1) // 2 if step % 2 else -(step // 2) for step in range(1, n)]
    by_offset = [None] * n
    for offset, block in zip(offsets, held):
        by_offset[offset % n] = block
    stacked = jnp.stack(by_offset)
    sources = jnp.arange(n, dtype=jnp.int32)
    return stacked[(index - sources) % n]


def local(inverse_factor, panel, trailing, extend_map):
    nrow = lax.axis_size("row")
    nz = lax.axis_size("z")
    ncore = lax.axis_size("core")
    ncol = nz * ncore
    group = nrow * ncol
    row_index = lax.axis_index("row")
    col_index = lax.axis_index("z") * ncore + lax.axis_index("core")

    inverse = lax.all_gather(inverse_factor[0], "core", axis=0, tiled=True)
    inverse = lax.all_gather(inverse, "z", axis=0, tiled=True)
    inverse = ring_gather(inverse, "row", row_index, nrow)
    order = inverse.shape[-1]
    inverse = inverse.reshape(order, order)

    columns = lax.all_gather(panel[0], ("z", "core"), axis=1, tiled=True)

    def solve(rows):
        return jnp.dot(rows, inverse, preferred_element_type=jnp.float32).astype(
            jnp.bfloat16
        )

    local_trailing = trailing[0]
    rows_here = local_trailing.shape[0]
    cols_here = local_trailing.shape[1]
    share = rows_here // ncol
    piece = solve(lax.dynamic_slice_in_dim(columns, col_index * share, share, 0))

    block_map = extend_map[0]
    nblocks = block_map.shape[0]
    per_class = nblocks // group
    width = rows_here // (ncol * per_class)
    slots_row = jnp.arange(ncol * per_class, dtype=jnp.int32)
    class_row = slots_row // per_class
    depth_row = slots_row % per_class
    source_row = (depth_row * ncol + class_row) * nrow + row_index
    target_row = class_row * per_class + block_map[source_row] // group
    gather_row = jnp.argsort(target_row)
    slots_col = jnp.arange(nrow * per_class, dtype=jnp.int32)
    class_col = slots_col // per_class
    depth_col = slots_col % per_class
    source_col = (depth_col * ncol + col_index) * nrow + class_col
    target_col = class_col * per_class + block_map[source_col] // group
    gather_col = jnp.argsort(target_col)

    own_blocks = (
        lax.dynamic_slice_in_dim(gather_col, row_index * per_class, per_class, 0)
        - row_index * per_class
    )
    copies = jnp.tile(own_blocks, nrow)
    piece = piece.reshape(per_class, width, order)[copies].reshape(nrow, share, order)
    col_side = lax.all_to_all(piece, "row", 0, 0, tiled=True).reshape(cols_here, order)
    lane = jnp.arange(cols_here, dtype=jnp.int32)
    picked = gather_col[lane // width] * width + lane % width
    select_cols = (lane[:, None] == picked[None, :]).astype(jnp.float32)

    solved = solve(columns)
    member = lax.axis_index("front") % 2
    half = rows_here // 2
    half_blocks = half // width

    def half_update(which, part, parts):
        size = half // parts
        first = which * half + part * size
        rows = lax.dynamic_slice_in_dim(local_trailing, first, size, 0)
        low = lax.dynamic_slice_in_dim(solved, first, size, 0)
        rows, low = lax.optimization_barrier((rows, low))
        moved_cols = jnp.dot(
            rows,
            select_cols,
            precision=lax.Precision.HIGHEST,
            preferred_element_type=jnp.float32,
        )
        schur = moved_cols - outer_rows(low, col_side)
        count = size // width
        blocks = (
            lax.dynamic_slice_in_dim(gather_row, first // width, count, 0)
            - first // width
        )
        return schur.reshape(count, width, cols_here)[blocks].reshape(size, cols_here)

    incoming = []
    for part in range(2):
        outgoing = half_update(1 - member, part, 2).astype(jnp.bfloat16)
        incoming.append(from_partner(outgoing, "front", 0))
    incoming = jnp.concatenate(incoming, axis=0)
    keep = half_update(member, 0, 1)
    return (keep + incoming.astype(jnp.float32))[None]


def solution(mesh):
    devices = mesh.devices
    shape = devices.shape
    fine = Mesh(
        devices.reshape(shape[0], shape[1], shape[2] // 2, 2),
        ("front", "row", "z", "core"),
    )
    cols = ("z", "core")
    return jax.shard_map(
        local,
        mesh=fine,
        in_specs=(
            P("front", ("row",) + cols, None),
            P("front", "row", cols),
            P("front", "row", cols),
            P("front", None),
        ),
        out_specs=P("front", "row", cols),
        check_vma=False,
    )
```

```python
import jax
import jax.numpy as jnp
from jax import lax
from jax.sharding import Mesh
from jax.sharding import PartitionSpec as P


def from_partner(value, axis, distance):
    mask = 2**distance
    pairs = [(source, source ^ mask) for source in range(lax.axis_size(axis))]
    return lax.ppermute(value, axis, pairs)


def outer_rows(left, right):
    return lax.dot_general(
        left, right, (((1,), (1,)), ((), ())), preferred_element_type=jnp.float32
    )


def ring_gather(value, axis, index, n):
    ahead = [(source, (source + 1) % n) for source in range(n)]
    behind = [(source, (source - 1) % n) for source in range(n)]
    held = [value]
    forward = value
    backward = value
    for step in range(1, n):
        if step % 2:
            forward = lax.ppermute(forward, axis, ahead)
            held.append(forward)
        else:
            backward = lax.ppermute(backward, axis, behind)
            held.append(backward)
    offsets = [0] + [(step + 1) // 2 if step % 2 else -(step // 2) for step in range(1, n)]
    by_offset = [None] * n
    for offset, block in zip(offsets, held):
        by_offset[offset % n] = block
    stacked = jnp.stack(by_offset)
    sources = jnp.arange(n, dtype=jnp.int32)
    return stacked[(index - sources) % n]


def local(inverse_factor, panel, trailing, extend_map):
    nrow = lax.axis_size("row")
    nz = lax.axis_size("z")
    ncore = lax.axis_size("core")
    ncol = nz * ncore
    group = nrow * ncol
    row_index = lax.axis_index("row")
    col_index = lax.axis_index("z") * ncore + lax.axis_index("core")

    inverse = lax.all_gather(inverse_factor[0], "core", axis=0, tiled=True)
    inverse = lax.all_gather(inverse, "z", axis=0, tiled=True)
    inverse = ring_gather(inverse, "row", row_index, nrow)
    order = inverse.shape[-1]
    inverse = inverse.reshape(order, order)

    columns = lax.all_gather(panel[0], ("z", "core"), axis=1, tiled=True)

    def solve(rows):
        return jnp.dot(rows, inverse, preferred_element_type=jnp.float32).astype(
            jnp.bfloat16
        )

    local_trailing = trailing[0]
    rows_here = local_trailing.shape[0]
    cols_here = local_trailing.shape[1]
    share = rows_here // ncol
    piece = solve(lax.dynamic_slice_in_dim(columns, col_index * share, share, 0))

    block_map = extend_map[0]
    nblocks = block_map.shape[0]
    per_class = nblocks // group
    width = rows_here // (ncol * per_class)
    slots_row = jnp.arange(ncol * per_class, dtype=jnp.int32)
    class_row = slots_row // per_class
    depth_row = slots_row % per_class
    source_row = (depth_row * ncol + class_row) * nrow + row_index
    target_row = class_row * per_class + block_map[source_row] // group
    gather_row = jnp.argsort(target_row)
    slots_col = jnp.arange(nrow * per_class, dtype=jnp.int32)
    class_col = slots_col // per_class
    depth_col = slots_col % per_class
    source_col = (depth_col * ncol + col_index) * nrow + class_col
    target_col = class_col * per_class + block_map[source_col] // group
    gather_col = jnp.argsort(target_col)

    own_blocks = (
        lax.dynamic_slice_in_dim(gather_col, row_index * per_class, per_class, 0)
        - row_index * per_class
    )
    copies = jnp.tile(own_blocks, nrow)
    piece = piece.reshape(per_class, width, order)[copies].reshape(nrow, share, order)
    col_side = lax.all_to_all(piece, "row", 0, 0, tiled=True).reshape(cols_here, order)
    lane = jnp.arange(cols_here, dtype=jnp.int32)
    picked = gather_col[lane // width] * width + lane % width
    select_cols = (lane[:, None] == picked[None, :]).astype(jnp.float32)

    solved = solve(columns)
    member = lax.axis_index("front") % 2
    half = rows_here // 2
    half_blocks = half // width

    nblocks_here = rows_here // width
    trailing_moved = local_trailing.reshape(nblocks_here, width, cols_here)[
        gather_row
    ].reshape(rows_here, cols_here)
    solved_blocks = solved.reshape(nblocks_here, width, order)

    def half_update(which):
        rows = lax.dynamic_slice_in_dim(trailing_moved, which * half, half, 0)
        blocks = lax.dynamic_slice_in_dim(gather_row, which * half_blocks, half_blocks, 0)
        low = solved_blocks[blocks].reshape(half, order)
        rows, low = lax.optimization_barrier((rows, low))
        moved_cols = jnp.dot(
            rows,
            select_cols,
            precision=lax.Precision.HIGHEST,
            preferred_element_type=jnp.float32,
        )
        return moved_cols - outer_rows(low, col_side)

    outgoing = half_update(1 - member).astype(jnp.bfloat16)
    incoming = from_partner(outgoing, "front", 0)
    keep = half_update(member)
    return (keep + incoming.astype(jnp.float32))[None]


def solution(mesh):
    devices = mesh.devices
    shape = devices.shape
    fine = Mesh(
        devices.reshape(shape[0], shape[1], shape[2] // 2, 2),
        ("front", "row", "z", "core"),
    )
    cols = ("z", "core")
    return jax.shard_map(
        local,
        mesh=fine,
        in_specs=(
            P("front", ("row",) + cols, None),
            P("front", "row", cols),
            P("front", "row", cols),
            P("front", None),
        ),
        out_specs=P("front", "row", cols),
        check_vma=False,
    )
```

```python
import jax
import jax.numpy as jnp
from jax import lax
from jax.sharding import Mesh
from jax.sharding import PartitionSpec as P


def from_partner(value, axis, distance):
    mask = 2**distance
    pairs = [(source, source ^ mask) for source in range(lax.axis_size(axis))]
    return lax.ppermute(value, axis, pairs)


def outer_rows(left, right):
    return lax.dot_general(
        left, right, (((1,), (1,)), ((), ())), preferred_element_type=jnp.float32
    )


def ring_gather(value, axis, index, n):
    ahead = [(source, (source + 1) % n) for source in range(n)]
    behind = [(source, (source - 1) % n) for source in range(n)]
    held = [value]
    forward = value
    backward = value
    for step in range(1, n):
        if step % 2:
            forward = lax.ppermute(forward, axis, ahead)
            held.append(forward)
        else:
            backward = lax.ppermute(backward, axis, behind)
            held.append(backward)
    offsets = [0] + [(step + 1) // 2 if step % 2 else -(step // 2) for step in range(1, n)]
    by_offset = [None] * n
    for offset, block in zip(offsets, held):
        by_offset[offset % n] = block
    stacked = jnp.stack(by_offset)
    sources = jnp.arange(n, dtype=jnp.int32)
    return stacked[(index - sources) % n]


def inverse_order(target):
    slots = jnp.arange(target.shape[0], dtype=jnp.int32)
    hit = target[None, :] == slots[:, None]
    return jnp.sum(jnp.where(hit, slots[None, :], 0), axis=1, dtype=jnp.int32)


def local(inverse_factor, panel, trailing, extend_map):
    nrow = lax.axis_size("row")
    nz = lax.axis_size("z")
    ncore = lax.axis_size("core")
    ncol = nz * ncore
    group = nrow * ncol
    row_index = lax.axis_index("row")
    col_index = lax.axis_index("z") * ncore + lax.axis_index("core")

    inverse = lax.all_gather(inverse_factor[0], "core", axis=0, tiled=True)
    inverse = lax.all_gather(inverse, "z", axis=0, tiled=True)
    inverse = ring_gather(inverse, "row", row_index, nrow)
    order = inverse.shape[-1]
    inverse = inverse.reshape(order, order)

    columns = lax.all_gather(panel[0], ("z", "core"), axis=1, tiled=True)

    def solve(rows):
        return jnp.dot(rows, inverse, preferred_element_type=jnp.float32).astype(
            jnp.bfloat16
        )

    local_trailing = trailing[0]
    rows_here = local_trailing.shape[0]
    cols_here = local_trailing.shape[1]
    share = rows_here // ncol
    piece = solve(lax.dynamic_slice_in_dim(columns, col_index * share, share, 0))

    block_map = extend_map[0]
    nblocks = block_map.shape[0]
    per_class = nblocks // group
    width = rows_here // (ncol * per_class)
    slots_row = jnp.arange(ncol * per_class, dtype=jnp.int32)
    class_row = slots_row // per_class
    depth_row = slots_row % per_class
    source_row = (depth_row * ncol + class_row) * nrow + row_index
    target_row = class_row * per_class + block_map[source_row] // group
    gather_row = inverse_order(target_row)
    slots_col = jnp.arange(nrow * per_class, dtype=jnp.int32)
    class_col = slots_col // per_class
    depth_col = slots_col % per_class
    source_col = (depth_col * ncol + col_index) * nrow + class_col
    target_col = class_col * per_class + block_map[source_col] // group
    gather_col = inverse_order(target_col)

    own_blocks = (
        lax.dynamic_slice_in_dim(gather_col, row_index * per_class, per_class, 0)
        - row_index * per_class
    )
    copies = jnp.tile(own_blocks, nrow)
    piece = piece.reshape(per_class, width, order)[copies].reshape(nrow, share, order)
    col_side = lax.all_to_all(piece, "row", 0, 0, tiled=True).reshape(cols_here, order)
    blocks_col = slots_col[:, None] == gather_col[None, :]
    same = jnp.arange(width)[:, None] == jnp.arange(width)[None, :]
    select_cols = (blocks_col[:, None, :, None] & same[None, :, None, :]).reshape(
        cols_here, cols_here
    ).astype(jnp.float32)

    solved = solve(columns)
    member = lax.axis_index("front") % 2
    half = rows_here // 2
    half_blocks = half // width

    def half_update(which):
        rows = lax.dynamic_slice_in_dim(local_trailing, which * half, half, 0)
        low = lax.dynamic_slice_in_dim(solved, which * half, half, 0)
        rows, low = lax.optimization_barrier((rows, low))
        moved_cols = jnp.dot(
            rows,
            select_cols,
            precision=lax.Precision.HIGHEST,
            preferred_element_type=jnp.float32,
        )
        schur = moved_cols - outer_rows(low, col_side)
        blocks = (
            lax.dynamic_slice_in_dim(gather_row, which * half_blocks, half_blocks, 0)
            - which * half_blocks
        )
        return schur.reshape(half_blocks, width, cols_here)[blocks].reshape(
            half, cols_here
        )

    outgoing = half_update(1 - member).astype(jnp.bfloat16)
    incoming = from_partner(outgoing, "front", 0)
    keep = half_update(member)
    return (keep + incoming.astype(jnp.float32))[None]


def solution(mesh):
    devices = mesh.devices
    shape = devices.shape
    fine = Mesh(
        devices.reshape(shape[0], shape[1], shape[2] // 2, 2),
        ("front", "row", "z", "core"),
    )
    cols = ("z", "core")
    return jax.shard_map(
        local,
        mesh=fine,
        in_specs=(
            P("front", ("row",) + cols, None),
            P("front", "row", cols),
            P("front", "row", cols),
            P("front", None),
        ),
        out_specs=P("front", "row", cols),
        check_vma=False,
    )
```

```python
import jax
import jax.numpy as jnp
from jax import lax
from jax.sharding import Mesh
from jax.sharding import PartitionSpec as P


def from_partner(value, axis, distance):
    mask = 2**distance
    pairs = [(source, source ^ mask) for source in range(lax.axis_size(axis))]
    return lax.ppermute(value, axis, pairs)


def outer_rows(left, right):
    return lax.dot_general(
        left, right, (((1,), (1,)), ((), ())), preferred_element_type=jnp.float32
    )


def direct_gather(value, axis, index, n):
    held = [value]
    for offset in range(1, n):
        pairs = [(source, (source + offset) % n) for source in range(n)]
        held.append(lax.ppermute(value, axis, pairs))
    stacked = jnp.stack(held)
    sources = jnp.arange(n, dtype=jnp.int32)
    return stacked[(index - sources) % n]


def inverse_order(target):
    slots = jnp.arange(target.shape[0], dtype=jnp.int32)
    hit = target[None, :] == slots[:, None]
    return jnp.sum(jnp.where(hit, slots[None, :], 0), axis=1, dtype=jnp.int32)


def local(inverse_factor, panel, trailing, extend_map):
    nrow = lax.axis_size("row")
    nz = lax.axis_size("z")
    ncore = lax.axis_size("core")
    ncol = nz * ncore
    group = nrow * ncol
    row_index = lax.axis_index("row")
    col_index = lax.axis_index("z") * ncore + lax.axis_index("core")

    inverse = lax.all_gather(inverse_factor[0], "core", axis=0, tiled=True)
    inverse = lax.all_gather(inverse, "z", axis=0, tiled=True)
    inverse = direct_gather(inverse, "row", row_index, nrow)
    order = inverse.shape[-1]
    inverse = inverse.reshape(order, order)

    columns = lax.all_gather(panel[0], ("z", "core"), axis=1, tiled=True)

    def solve(rows):
        return jnp.dot(rows, inverse, preferred_element_type=jnp.float32).astype(
            jnp.bfloat16
        )

    local_trailing = trailing[0]
    rows_here = local_trailing.shape[0]
    cols_here = local_trailing.shape[1]
    share = rows_here // ncol
    piece = solve(lax.dynamic_slice_in_dim(columns, col_index * share, share, 0))

    block_map = extend_map[0]
    nblocks = block_map.shape[0]
    per_class = nblocks // group
    width = rows_here // (ncol * per_class)
    slots_row = jnp.arange(ncol * per_class, dtype=jnp.int32)
    class_row = slots_row // per_class
    depth_row = slots_row % per_class
    source_row = (depth_row * ncol + class_row) * nrow + row_index
    target_row = class_row * per_class + block_map[source_row] // group
    gather_row = inverse_order(target_row)
    slots_col = jnp.arange(nrow * per_class, dtype=jnp.int32)
    class_col = slots_col // per_class
    depth_col = slots_col % per_class
    source_col = (depth_col * ncol + col_index) * nrow + class_col
    target_col = class_col * per_class + block_map[source_col] // group
    gather_col = inverse_order(target_col)

    own_blocks = (
        lax.dynamic_slice_in_dim(gather_col, row_index * per_class, per_class, 0)
        - row_index * per_class
    )
    copies = jnp.tile(own_blocks, nrow)
    piece = piece.reshape(per_class, width, order)[copies].reshape(nrow, share, order)
    col_side = lax.all_to_all(piece, "row", 0, 0, tiled=True).reshape(cols_here, order)
    blocks_col = slots_col[:, None] == gather_col[None, :]
    same = jnp.arange(width)[:, None] == jnp.arange(width)[None, :]
    select_cols = (blocks_col[:, None, :, None] & same[None, :, None, :]).reshape(
        cols_here, cols_here
    ).astype(jnp.float32)

    solved = solve(columns)
    member = lax.axis_index("front") % 2
    half = rows_here // 2
    half_blocks = half // width

    def half_update(which):
        rows = lax.dynamic_slice_in_dim(local_trailing, which * half, half, 0)
        low = lax.dynamic_slice_in_dim(solved, which * half, half, 0)
        rows, low = lax.optimization_barrier((rows, low))
        moved_cols = jnp.dot(
            rows,
            select_cols,
            precision=lax.Precision.HIGHEST,
            preferred_element_type=jnp.float32,
        )
        schur = moved_cols - outer_rows(low, col_side)
        blocks = (
            lax.dynamic_slice_in_dim(gather_row, which * half_blocks, half_blocks, 0)
            - which * half_blocks
        )
        return schur.reshape(half_blocks, width, cols_here)[blocks].reshape(
            half, cols_here
        )

    outgoing = half_update(1 - member).astype(jnp.bfloat16)
    incoming = from_partner(outgoing, "front", 0)
    keep = half_update(member)
    return (keep + incoming.astype(jnp.float32))[None]


def solution(mesh):
    devices = mesh.devices
    shape = devices.shape
    fine = Mesh(
        devices.reshape(shape[0], shape[1], shape[2] // 2, 2),
        ("front", "row", "z", "core"),
    )
    cols = ("z", "core")
    return jax.shard_map(
        local,
        mesh=fine,
        in_specs=(
            P("front", ("row",) + cols, None),
            P("front", "row", cols),
            P("front", "row", cols),
            P("front", None),
        ),
        out_specs=P("front", "row", cols),
        check_vma=False,
    )
```
